256 devices in a mesh: heads: 4 (over x), seq: 64 (over z, y, core).
Axes of the slice: x: 4, y: 4, z: 8, core: 2. Of those that a mesh axis runs over, the one named last changes fastest.
Arguments:
- queries: bfloat16 [32768, 2048], P('seq', 'heads'), may hold values from -64 to 64
- keys: bfloat16 [32768, 512], P('seq', 'heads'), may hold values from -6 to 6
- values: bfloat16 [32768, 512], P('seq', 'heads'), may hold values from -6 to 6
- vertical: int32 [16, 16], replicated, may hold values from 0 to 511, as said below
- slash: int32 [16, 8], replicated, may hold values from 0 to 15, as said below
- out_weight: bfloat16 [2048, 4096], P('heads'), may hold values from -0.25 to 0.25
Outputs:
- layer_out: bfloat16 [32768, 4096], P('seq', 'heads')
The draws below stay inside these ranges and needn't reach their ends.
Inputs may be any that keep to these rules, and one draw needn't show every extreme that they name: `vertical`: each row lists 16 distinct blocks; the four rows of one KV head (rows 4g to 4g+3) list 64 distinct blocks in all; at most 2 of those lie within blocks k * 8 to (k + 1) * 8 - 1 for any k, and in every draw some k reaches 2. `slash`: each row lists 8 distinct offsets, 0 among them; some row holds 15 in every draw.
All inputs are finite; a program needn't handle non-finite values.
Results may differ from the reference program's by a relative error of at most 0.0095.
Values may be sent and summed in bfloat16 or wider, within the bound.
No kernel may reach another device: no remote copies, remote signals or barrier semaphores. Data moves between devices by JAX's collectives and lax.ppermute only.
A program may use at most 128 MiB of HBM per device.

```python
import math
import jax
import jax.numpy as jnp
from jax import lax

D = 4096
HEAD_SIZE = 128
BLOCK_TOKENS = 64
VERTICAL_COUNT = 16
NS = 8
KEY_VALUE_HEADS = 4
QUERY_HEADS = 16
BLK_DEV = 8
SEQUENCE_TOKENS = 32768
NB = 512
U = 64
MV = 2


def joint_draw(key):
    base = jax.random.fold_in(key, 11)
    random_key_first, key_b = jax.random.split(base, 2)
    key_entries = jnp.clip(jax.random.normal(random_key_first, (SEQUENCE_TOKENS, KEY_VALUE_HEADS * HEAD_SIZE)), -6.0, 6.0)
    query_vals = 1.5 * jnp.clip(jax.random.normal(key_b, (SEQUENCE_TOKENS, QUERY_HEADS * HEAD_SIZE)), -6.0, 6.0)
    return (query_vals, key_entries)


def draw_queries(key, part):
    query_vals, key_entries = joint_draw(key)
    return query_vals.astype(jnp.float32).astype(jnp.bfloat16)


def draw_keys(key, part):
    query_vals, key_entries = joint_draw(key)
    return key_entries.astype(jnp.float32).astype(jnp.bfloat16)


def draw_vertical(key, part):
    ranges = NB // BLK_DEV
    span = BLK_DEV // MV
    output_rows = []
    for index_in_group in range(KEY_VALUE_HEADS):
        group_key = jax.random.fold_in(key, 100 + index_in_group)
        key_one, key_two, random_key_third, key_four = jax.random.split(group_key, 4)
        full_range = jax.random.randint(key_one, (), 0, ranges)
        others = jax.random.permutation(key_two, (ranges - 1) * MV)[:U - MV]
        other_range = others // MV
        other_range = other_range + (other_range >= full_range).astype(jnp.int32)
        other_pos = others % MV
        range_all = jnp.concatenate([jnp.full((MV,), full_range, jnp.int32), other_range.astype(jnp.int32)])
        pos_all = jnp.concatenate([jnp.arange(MV, dtype=jnp.int32), other_pos.astype(jnp.int32)])
        block_list = range_all * BLK_DEV + pos_all * span + jax.random.randint(random_key_third, (U,), 0, span)
        random_order = jax.random.permutation(key_four, U)
        output_rows.append(block_list[random_order].reshape(QUERY_HEADS // KEY_VALUE_HEADS, VERTICAL_COUNT))
    return jnp.concatenate(output_rows, axis=0).astype(jnp.int32)


def draw_slash(key, part):
    far_row = jax.random.randint(jax.random.fold_in(key, 500), (), 0, QUERY_HEADS)
    output_rows = []
    for row_index in range(QUERY_HEADS):
        perm = jax.random.permutation(jax.random.fold_in(key, 600 + row_index), 2 * BLK_DEV - 2) + 1
        last = jnp.where(row_index == far_row, 2 * BLK_DEV - 1, perm[NS - 2])
        row = jnp.concatenate([jnp.zeros((1,), jnp.int32), perm[:NS - 2].astype(jnp.int32), jnp.reshape(last, (1,)).astype(jnp.int32)])
        output_rows.append(row)
    return jnp.stack(output_rows).astype(jnp.int32)


def block_levels(key, shape, cuts, smallest, top_value):
    loudness, own = 1.0, jax.random.fold_in(key, 6)
    for axis_at, blocks in cuts:
        steps = jnp.exp(jax.random.uniform(jax.random.fold_in(own, axis_at), (blocks,), jnp.float32, smallest / len(cuts), top_value / len(cuts)))
        loudness = loudness * jnp.repeat(steps, shape[axis_at] // blocks).reshape([-1 if axis == axis_at else 1 for axis in range(len(shape))])
    return loudness


def noise(stream_key, shape, deviation, reach, cuts=(), kind=jnp.bfloat16):
    factor_of = block_levels(stream_key, shape, cuts, -0.22, 0.18) if cuts else 1.0
    values = jax.random.normal(stream_key, shape, jnp.float32) * deviation * factor_of
    return jnp.minimum(jnp.maximum(values, -reach), reach).astype(kind)


def setup_inputs(seed: int = 0) -> dict:
    arg_keys = jax.random.split(jax.random.key(seed), 7)
    queries = draw_queries(jax.random.fold_in(arg_keys[6], 71), 0)
    keys = draw_keys(jax.random.fold_in(arg_keys[6], 71), 0)
    values = noise(arg_keys[2], (SEQUENCE_TOKENS, KEY_VALUE_HEADS * HEAD_SIZE), 1.0, 6.0, ((0, 64), (1, 4)))
    vertical = draw_vertical(jax.random.fold_in(arg_keys[6], 71), 0)
    slash = draw_slash(jax.random.fold_in(arg_keys[6], 71), 0)
    out_weight = noise(arg_keys[5], (QUERY_HEADS * HEAD_SIZE, D), (4 * HEAD_SIZE) ** -0.5, 0.25, ((0, 4),))
    return dict(queries=queries, keys=keys, values=values, vertical=vertical, slash=slash, out_weight=out_weight)


def reference(queries, keys, values, vertical, slash, out_weight):
    token_count = queries.shape[0]
    total_blocks = token_count // BLOCK_TOKENS
    heads_per_group = QUERY_HEADS // KEY_VALUE_HEADS
    score_scale = 1.0 / math.sqrt(HEAD_SIZE)
    query_all = queries.reshape(total_blocks, BLOCK_TOKENS, QUERY_HEADS, HEAD_SIZE)
    key_head_rows = keys.reshape(total_blocks, BLOCK_TOKENS, KEY_VALUE_HEADS, HEAD_SIZE).transpose(2, 0, 1, 3)
    value_head_rows = values.reshape(total_blocks, BLOCK_TOKENS, KEY_VALUE_HEADS, HEAD_SIZE).transpose(2, 0, 1, 3)
    owner_head = (jnp.arange(QUERY_HEADS) // heads_per_group).astype(jnp.int32)
    token_pos = jnp.arange(BLOCK_TOKENS)
    causal_tri = token_pos[None, :] <= token_pos[:, None]
    vert_keys = key_head_rows[owner_head[:, None], vertical].astype(jnp.float32)
    vert_values = value_head_rows[owner_head[:, None], vertical].astype(jnp.float32)

    def one_block(block_index):
        query_rows = query_all[block_index].astype(jnp.float32)
        target = block_index - slash
        listed = jnp.any(vertical[:, :, None] == target[:, None, :], axis=1)
        keep = (target >= 0) & jnp.logical_not(listed)
        safe_target = jnp.maximum(target, 0).astype(jnp.int32)
        diag_keys = key_head_rows[owner_head[:, None], safe_target].astype(jnp.float32)
        diag_values = value_head_rows[owner_head[:, None], safe_target].astype(jnp.float32)
        score_vert = jnp.einsum('bhd,hnkd->bhnk', query_rows, vert_keys) * score_scale
        score_diag = jnp.einsum('bhd,hnkd->bhnk', query_rows, diag_keys) * score_scale
        allow_vert = (vertical < block_index)[None, :, :, None] | (vertical == block_index)[None, :, :, None] & causal_tri[:, None, None, :]
        allow_diag = keep[None, :, :, None] & ((slash != 0)[None, :, :, None] | causal_tri[:, None, None, :])
        scores = jnp.concatenate([score_vert.reshape(BLOCK_TOKENS, QUERY_HEADS, -1), score_diag.reshape(BLOCK_TOKENS, QUERY_HEADS, -1)], axis=2)
        allowed = jnp.concatenate([allow_vert.reshape(BLOCK_TOKENS, QUERY_HEADS, -1), allow_diag.reshape(BLOCK_TOKENS, QUERY_HEADS, -1)], axis=2)
        row_top = lax.optimization_barrier(jnp.max(jnp.where(allowed, scores, -jnp.inf), axis=2, keepdims=True))
        expo = jnp.where(allowed, jnp.exp(scores - row_top), 0.0)
        row_total = lax.optimization_barrier(jnp.sum(expo, axis=2, keepdims=True))
        weights = (expo / row_total).astype(jnp.bfloat16).astype(jnp.float32)
        split_at = vertical.shape[1] * BLOCK_TOKENS
        weight_vert = weights[:, :, :split_at].reshape(BLOCK_TOKENS, QUERY_HEADS, -1, BLOCK_TOKENS)
        weight_diag = weights[:, :, split_at:].reshape(BLOCK_TOKENS, QUERY_HEADS, -1, BLOCK_TOKENS)
        result = jnp.einsum('bhnk,hnkd->bhd', weight_vert, vert_values) + jnp.einsum('bhnk,hnkd->bhd', weight_diag, diag_values)
        return result.astype(jnp.bfloat16)
    attention = lax.map(one_block, jnp.arange(total_blocks).astype(jnp.int32))
    attention = attention.reshape(token_count, QUERY_HEADS * HEAD_SIZE)
    group_width = heads_per_group * HEAD_SIZE
    summed = jnp.zeros((token_count, out_weight.shape[1]), jnp.float32)
    for index_in_group in range(KEY_VALUE_HEADS):
        lo_col = index_in_group * group_width
        part = jnp.dot(attention[:, lo_col:lo_col + group_width], out_weight[lo_col:lo_col + group_width], preferred_element_type=jnp.float32).astype(jnp.bfloat16)
        summed = summed + lax.optimization_barrier(part).astype(jnp.float32)
    return summed.astype(jnp.bfloat16)
```

```python
import math

import jax
import jax.numpy as jnp
import numpy as np
from jax import lax
from jax.sharding import Mesh
from jax.sharding import PartitionSpec as P

HEAD_SIZE = 128
BLOCK_TOKENS = 64
SEQ = ("z", "y", "core")
PLANE = ("z", "y")


def shift(block, axis, size, distance):
    route = [(i, i + distance) for i in range(size) if 0 <= i + distance < size]
    return lax.ppermute(block, axis, route)


def ring(block, axis, size, distance):
    return lax.ppermute(block, axis, [(i, (i + distance) % size) for i in range(size)])


def attend_head(query_rows, vert_pair, context, vert_blocks, offsets, first_block):
    block_count = context.shape[1] // 3
    head_dim = query_rows.shape[1]
    score_scale = 1.0 / math.sqrt(head_dim)
    block_rows = query_rows.reshape(block_count, BLOCK_TOKENS, head_dim)
    near_pair = jax.vmap(
        lambda offset: lax.dynamic_slice_in_dim(context, 2 * block_count - offset, block_count, 1)
    )(offsets)
    score_vert = (
        jnp.einsum("abd,nkd->abnk", block_rows, vert_pair[0], preferred_element_type=jnp.float32)
        * score_scale
    )
    score_diag = (
        jnp.einsum(
            "abd,nakd->abnk", block_rows, near_pair[:, 0], preferred_element_type=jnp.float32
        )
        * score_scale
    )
    query_block = first_block + jnp.arange(block_count, dtype=jnp.int32)
    token_pos = jnp.arange(BLOCK_TOKENS)
    causal_tri = token_pos[None, :] <= token_pos[:, None]
    vert_here = vert_blocks[None, None, :, None]
    block_here = query_block[:, None, None, None]
    allow_vert = (vert_here < block_here) | (vert_here == block_here) & causal_tri[None, :, None, :]
    target = query_block[None, :] - offsets[:, None]
    listed = jnp.any(vert_blocks[:, None, None] == target[None, :, :], axis=0)
    keep = (target >= 0) & jnp.logical_not(listed)
    allow_diag = keep.T[:, None, :, None] & (
        (offsets != 0)[None, None, :, None] | causal_tri[None, :, None, :]
    )
    top_vert = jnp.max(jnp.where(allow_vert, score_vert, -jnp.inf), axis=(2, 3), keepdims=True)
    top_diag = jnp.max(jnp.where(allow_diag, score_diag, -jnp.inf), axis=(2, 3), keepdims=True)
    row_top = jnp.maximum(top_vert, top_diag)
    expo_vert = jnp.where(allow_vert, jnp.exp(score_vert - row_top), 0.0)
    expo_diag = jnp.where(allow_diag, jnp.exp(score_diag - row_top), 0.0)
    row_total = jnp.sum(expo_vert, axis=(2, 3), keepdims=True) + jnp.sum(
        expo_diag, axis=(2, 3), keepdims=True
    )
    weight_vert = (expo_vert / row_total).astype(jnp.bfloat16)
    weight_diag = (expo_diag / row_total).astype(jnp.bfloat16)
    result = jnp.einsum(
        "abnk,nkd->abd", weight_vert, vert_pair[1], preferred_element_type=jnp.float32
    )
    result = result + jnp.einsum(
        "abnk,nakd->abd", weight_diag, near_pair[:, 1], preferred_element_type=jnp.float32
    )
    return result.reshape(block_count * BLOCK_TOKENS, head_dim).astype(jnp.bfloat16)


def make_local(sizes):
    heads_n, z_n, y_n, core_n = sizes
    cycle_size = z_n * y_n * core_n
    plane_size = z_n * y_n

    def local(queries, keys, values, vertical, slash, out_weight):
        head_dim = HEAD_SIZE
        local_heads = queries.shape[1] // head_dim
        token_count = queries.shape[0]
        block_count = token_count // BLOCK_TOKENS
        kv_group = lax.axis_index("heads")
        core = lax.axis_index("core")
        cycle_index = lax.axis_index(SEQ)

        rows_total, width = out_weight.shape
        col_width = width // heads_n
        half_rows = rows_total // core_n
        fetched = []
        for distance in range(1, heads_n):
            dest_cols = ((kv_group + distance) % heads_n) * col_width
            piece = lax.dynamic_slice(out_weight, (core * half_rows, dest_cols), (half_rows, col_width))
            fetched.append(ring(piece, "heads", heads_n, distance))
        fetched = jnp.stack(fetched)
        sibling_w = ring(fetched, "core", core_n, 1)
        own_w = lax.dynamic_slice(out_weight, (0, kv_group * col_width), (rows_total, col_width))

        vert_group = lax.dynamic_slice_in_dim(vertical, kv_group * local_heads, local_heads, 0)
        slash_group = lax.dynamic_slice_in_dim(slash, kv_group * local_heads, local_heads, 0)
        union_list = vert_group.reshape(-1)
        listed_count = union_list.shape[0]
        owner_dev = union_list // block_count
        within_dev = union_list % block_count
        paired = jnp.stack([keys, values]).reshape(2, block_count, BLOCK_TOKENS, head_dim)
        owned_here = owner_dev == cycle_index
        capacity = min(block_count, max(2, 2 * listed_count // cycle_size))
        positions = jnp.arange(listed_count)
        same_owner = (owner_dev[:, None] == owner_dev[None, :]) & (
            positions[None, :] < positions[:, None]
        )
        slot_index = jnp.sum(same_owner.astype(jnp.int32), axis=1)
        selector = owned_here[None, :] & (slot_index[None, :] == jnp.arange(capacity)[:, None])
        picked = jnp.sum(jnp.where(selector, within_dev[None, :], 0), axis=1)
        outgoing = paired[:, picked]
        gathered = lax.all_gather(outgoing, PLANE, axis=0, tiled=False)
        sibling = ring(gathered, "core", core_n, 1)
        both = jnp.stack([gathered, sibling])
        owner_plane = owner_dev // core_n
        from_sibling = (owner_dev % core_n != core).astype(jnp.int32)
        chosen = both[from_sibling, owner_plane, :, slot_index]
        chosen = chosen.reshape(local_heads, vert_group.shape[1], 2, BLOCK_TOKENS, head_dim)
        chosen = jnp.moveaxis(chosen, 2, 0)
        earlier = shift(paired, SEQ, cycle_size, 1)
        farther = shift(paired, SEQ, cycle_size, 2)
        context = jnp.concatenate([farther, earlier, paired], axis=1)
        first_block = cycle_index * block_count
        outputs = []
        for head_index in range(local_heads):
            query_rows = queries[:, head_index * head_dim : (head_index + 1) * head_dim]
            outputs.append(
                attend_head(
                    query_rows,
                    chosen[:, head_index],
                    context,
                    vert_group[head_index],
                    slash_group[head_index],
                    first_block,
                )
            )
        attention = jnp.concatenate(outputs, axis=1)

        total = jnp.dot(attention, own_w, preferred_element_type=jnp.float32)
        for distance in range(1, heads_n):
            other = ring(attention, "heads", heads_n, distance)
            mine = lax.dynamic_slice_in_dim(other, core * half_rows, half_rows, 1)
            theirs = lax.dynamic_slice_in_dim(other, (1 - core) * half_rows, half_rows, 1)
            total = total + jnp.dot(
                mine, fetched[distance - 1], preferred_element_type=jnp.float32
            )
            total = total + jnp.dot(
                theirs, sibling_w[distance - 1], preferred_element_type=jnp.float32
            )
        return total.astype(jnp.bfloat16)

    return local


def split_mesh(mesh):
    devices = mesh.devices
    heads_n, seq_n = devices.shape
    core_n = 2
    y_n = len({d.coords[1] for d in devices.flat})
    z_n = seq_n // (core_n * y_n)
    sizes = (heads_n, z_n, y_n, core_n)
    return Mesh(np.asarray(devices).reshape(sizes), ("heads",) + SEQ), sizes


def solution(mesh):
    sub, sizes = split_mesh(mesh)
    return jax.shard_map(
        make_local(sizes),
        mesh=sub,
        in_specs=(
            P(SEQ, "heads"),
            P(SEQ, "heads"),
            P(SEQ, "heads"),
            P(),
            P(),
            P("heads", None),
        ),
        out_specs=P(SEQ, "heads"),
        check_vma=False,
    )
```

```python
import math

import jax
import jax.numpy as jnp
import numpy as np
from jax import lax
from jax.sharding import Mesh
from jax.sharding import PartitionSpec as P

HEAD_SIZE = 128
BLOCK_TOKENS = 64
SEQ = ("z", "y", "core")


def shift(block, axis, size, distance):
    route = [(i, i + distance) for i in range(size) if 0 <= i + distance < size]
    return lax.ppermute(block, axis, route)


def ring(block, axis, size, distance):
    return lax.ppermute(block, axis, [(i, (i + distance) % size) for i in range(size)])


def spread(table, rows, cols):
    return jnp.repeat(jnp.repeat(table, rows, axis=-2), cols, axis=-1)


def make_local(sizes):
    heads_n, z_n, y_n, core_n = sizes
    cycle_size = z_n * y_n * core_n

    def local(queries, keys, values, vertical, slash, out_weight):
        head_dim = HEAD_SIZE
        local_heads = queries.shape[1] // head_dim
        token_count = queries.shape[0]
        block_count = token_count // BLOCK_TOKENS
        score_scale = 1.0 / math.sqrt(head_dim)
        kv_group = lax.axis_index("heads")
        core = lax.axis_index("core")
        cycle_index = lax.axis_index(SEQ)

        vert_group = lax.dynamic_slice_in_dim(vertical, kv_group * local_heads, local_heads, 0)
        slash_group = lax.dynamic_slice_in_dim(slash, kv_group * local_heads, local_heads, 0)
        union_list = vert_group.reshape(-1)
        listed_count = union_list.shape[0]
        owner_dev = union_list // block_count
        within_dev = union_list % block_count
        paired = jnp.stack([keys, values]).reshape(2, block_count, BLOCK_TOKENS, head_dim)
        owned_here = owner_dev == cycle_index
        capacity = min(block_count, max(2, 2 * listed_count // cycle_size))
        positions = jnp.arange(listed_count)
        same_owner = (owner_dev[:, None] == owner_dev[None, :]) & (
            positions[None, :] < positions[:, None]
        )
        slot_index = jnp.sum(same_owner.astype(jnp.int32), axis=1)
        selector = owned_here[None, :] & (slot_index[None, :] == jnp.arange(capacity)[:, None])
        picked = jnp.sum(jnp.where(selector, within_dev[None, :], 0), axis=1)
        outgoing = paired[:, picked].reshape(2, capacity * BLOCK_TOKENS, head_dim)
        arrived = lax.all_gather(outgoing, SEQ, axis=1, tiled=True)

        rows_total, width = out_weight.shape
        col_width = width // heads_n
        half_rows = rows_total // core_n
        fetched = []
        for distance in range(1, heads_n):
            dest_cols = ((kv_group + distance) % heads_n) * col_width
            piece = lax.dynamic_slice(out_weight, (core * half_rows, dest_cols), (half_rows, col_width))
            fetched.append(ring(piece, "heads", heads_n, distance))
        fetched = jnp.stack(fetched)
        sibling_w = ring(fetched, "core", core_n, 1)
        own_w = lax.dynamic_slice(out_weight, (0, kv_group * col_width), (rows_total, col_width))

        earlier = shift(paired, SEQ, cycle_size, 1)
        farther = shift(paired, SEQ, cycle_size, 2)
        context = jnp.concatenate([farther, earlier, paired], axis=1)
        context_blocks = context.shape[1]
        context_k = context[0].reshape(context_blocks * BLOCK_TOKENS, head_dim)
        context_v = context[1].reshape(context_blocks * BLOCK_TOKENS, head_dim)
        first_block = cycle_index * block_count
        query_block = first_block + jnp.arange(block_count, dtype=jnp.int32)
        key_block = first_block - (context_blocks - block_count) + jnp.arange(
            context_blocks, dtype=jnp.int32
        )
        distance_blk = query_block[:, None] - key_block[None, :]
        token_pos = jnp.arange(BLOCK_TOKENS)
        causal_tri = token_pos[None, :] <= token_pos[:, None]
        causal_ctx = jnp.tile(causal_tri, (block_count, context_blocks))

        query_heads = queries.reshape(token_count, local_heads, head_dim).transpose(1, 0, 2)
        score_diag = (
            jnp.einsum("htd,ud->htu", query_heads, context_k, preferred_element_type=jnp.float32)
            * score_scale
        )
        in_slash = jnp.any(distance_blk[None, None] == slash_group[:, :, None, None], axis=1)
        in_vert = jnp.any(key_block[None, None, :] == vert_group[:, :, None], axis=1)
        keep_blk = in_slash & (key_block >= 0)[None, None, :] & jnp.logical_not(in_vert)[:, None, :]
        whole_blk = keep_blk & (distance_blk != 0)[None]
        allow_diag = spread(whole_blk, BLOCK_TOKENS, BLOCK_TOKENS) | (
            spread(keep_blk & (distance_blk == 0)[None], BLOCK_TOKENS, BLOCK_TOKENS)
            & causal_ctx[None]
        )
        top_diag = jnp.max(jnp.where(allow_diag, score_diag, -jnp.inf), axis=2, keepdims=True)
        expo_diag = jnp.where(allow_diag, jnp.exp(score_diag - top_diag), 0.0)
        total_diag = jnp.sum(expo_diag, axis=2, keepdims=True)
        acc_diag = jnp.einsum(
            "htu,ud->htd",
            expo_diag.astype(jnp.bfloat16),
            context_v,
            preferred_element_type=jnp.float32,
        )

        arrived = arrived.reshape(2, cycle_size * capacity, BLOCK_TOKENS, head_dim)
        chosen = arrived[:, owner_dev * capacity + slot_index]
        vert_count = vert_group.shape[1]
        chosen = chosen.reshape(2, local_heads, vert_count * BLOCK_TOKENS, head_dim)
        score_vert = (
            jnp.einsum("htd,hud->htu", query_heads, chosen[0], preferred_element_type=jnp.float32)
            * score_scale
        )
        vert_cols = jnp.repeat(vert_group, BLOCK_TOKENS, axis=1)
        row_block = jnp.repeat(query_block, BLOCK_TOKENS)
        causal_vert = jnp.tile(causal_tri, (block_count, vert_count))
        allow_vert = (vert_cols[:, None, :] < row_block[None, :, None]) | (
            (vert_cols[:, None, :] == row_block[None, :, None]) & causal_vert[None]
        )
        top_vert = jnp.max(jnp.where(allow_vert, score_vert, -jnp.inf), axis=2, keepdims=True)
        row_top = jnp.maximum(top_diag, top_vert)
        expo_vert = jnp.where(allow_vert, jnp.exp(score_vert - row_top), 0.0)
        diag_scale = jnp.exp(top_diag - row_top)
        row_total = total_diag * diag_scale + jnp.sum(expo_vert, axis=2, keepdims=True)
        acc_vert = jnp.einsum(
            "htu,hud->htd",
            expo_vert.astype(jnp.bfloat16),
            chosen[1],
            preferred_element_type=jnp.float32,
        )
        head_out = (acc_diag * diag_scale + acc_vert) / row_total
        attention = head_out.astype(jnp.bfloat16).transpose(1, 0, 2).reshape(token_count, -1)

        total = jnp.dot(attention, own_w, preferred_element_type=jnp.float32)
        for distance in range(1, heads_n):
            other = ring(attention, "heads", heads_n, distance)
            mine = lax.dynamic_slice_in_dim(other, core * half_rows, half_rows, 1)
            theirs = lax.dynamic_slice_in_dim(other, (1 - core) * half_rows, half_rows, 1)
            total = total + jnp.dot(
                mine, fetched[distance - 1], preferred_element_type=jnp.float32
            )
            total = total + jnp.dot(
                theirs, sibling_w[distance - 1], preferred_element_type=jnp.float32
            )
        return total.astype(jnp.bfloat16)

    return local


def split_mesh(mesh):
    devices = mesh.devices
    heads_n, seq_n = devices.shape
    core_n = 2
    y_n = len({d.coords[1] for d in devices.flat})
    z_n = seq_n // (core_n * y_n)
    sizes = (heads_n, z_n, y_n, core_n)
    return Mesh(np.asarray(devices).reshape(sizes), ("heads",) + SEQ), sizes


def solution(mesh):
    sub, sizes = split_mesh(mesh)
    return jax.shard_map(
        make_local(sizes),
        mesh=sub,
        in_specs=(
            P(SEQ, "heads"),
            P(SEQ, "heads"),
            P(SEQ, "heads"),
            P(),
            P(),
            P("heads", None),
        ),
        out_specs=P(SEQ, "heads"),
        check_vma=False,
    )
```

```python
import math

import jax
import jax.numpy as jnp
import numpy as np
from jax import lax
from jax.sharding import Mesh
from jax.sharding import PartitionSpec as P

HEAD_SIZE = 128
BLOCK_TOKENS = 64
SEQ = ("z", "y", "core")


def shift(block, axis, size, distance):
    route = [(i, i + distance) for i in range(size) if 0 <= i + distance < size]
    return lax.ppermute(block, axis, route)


def ring(block, axis, size, distance):
    return lax.ppermute(block, axis, [(i, (i + distance) % size) for i in range(size)])


def spread(table, rows, cols):
    return jnp.repeat(jnp.repeat(table, rows, axis=-2), cols, axis=-1)


def make_local(sizes):
    heads_n, z_n, y_n, core_n = sizes
    cycle_size = z_n * y_n * core_n

    def local(queries, keys, values, vertical, slash, out_weight):
        head_dim = HEAD_SIZE
        local_heads = queries.shape[1] // head_dim
        token_count = queries.shape[0]
        block_count = token_count // BLOCK_TOKENS
        score_scale = 1.0 / math.sqrt(head_dim)
        kv_group = lax.axis_index("heads")
        core = lax.axis_index("core")
        cycle_index = lax.axis_index(SEQ)

        vert_group = lax.dynamic_slice_in_dim(vertical, kv_group * local_heads, local_heads, 0)
        slash_group = lax.dynamic_slice_in_dim(slash, kv_group * local_heads, local_heads, 0)
        union_list = vert_group.reshape(-1)
        listed_count = union_list.shape[0]
        owner_dev = union_list // block_count
        within_dev = union_list % block_count
        paired = jnp.stack([keys, values]).reshape(2, block_count, BLOCK_TOKENS, head_dim)
        owned_here = owner_dev == cycle_index
        capacity = min(block_count, max(2, 2 * listed_count // cycle_size))
        positions = jnp.arange(listed_count)
        same_owner = (owner_dev[:, None] == owner_dev[None, :]) & (
            positions[None, :] < positions[:, None]
        )
        slot_index = jnp.sum(same_owner.astype(jnp.int32), axis=1)
        selector = owned_here[None, :] & (slot_index[None, :] == jnp.arange(capacity)[:, None])
        picked = jnp.sum(jnp.where(selector, within_dev[None, :], 0), axis=1)
        outgoing = paired[:, picked].reshape(2, capacity * BLOCK_TOKENS, head_dim)
        arrived = lax.all_gather(outgoing, SEQ, axis=1, tiled=True)

        rows_total, width = out_weight.shape
        col_width = width // heads_n
        half_rows = rows_total // core_n
        fetched = []
        for distance in range(1, heads_n):
            dest_cols = ((kv_group + distance) % heads_n) * col_width
            piece = lax.dynamic_slice(out_weight, (core * half_rows, dest_cols), (half_rows, col_width))
            fetched.append(ring(piece, "heads", heads_n, distance))
        fetched = jnp.stack(fetched)
        sibling_w = ring(fetched, "core", core_n, 1)
        own_w = lax.dynamic_slice(out_weight, (0, kv_group * col_width), (rows_total, col_width))

        earlier = shift(paired, SEQ, cycle_size, 1)
        farther = shift(paired, SEQ, cycle_size, 2)
        context = jnp.concatenate([farther, earlier, paired], axis=1)
        context_blocks = context.shape[1]
        context_k = context[0].reshape(context_blocks * BLOCK_TOKENS, head_dim)
        context_v = context[1].reshape(context_blocks * BLOCK_TOKENS, head_dim)
        first_block = cycle_index * block_count
        query_block = first_block + jnp.arange(block_count, dtype=jnp.int32)
        key_block = first_block - (context_blocks - block_count) + jnp.arange(
            context_blocks, dtype=jnp.int32
        )
        distance_blk = query_block[:, None] - key_block[None, :]
        token_pos = jnp.arange(BLOCK_TOKENS)
        causal_tri = token_pos[None, :] <= token_pos[:, None]
        causal_ctx = jnp.tile(causal_tri, (block_count, context_blocks))

        query_heads = queries.reshape(token_count, local_heads, head_dim).transpose(1, 0, 2)
        score_diag = (
            jnp.einsum("htd,ud->htu", query_heads, context_k, preferred_element_type=jnp.float32)
            * score_scale
        )
        in_slash = jnp.any(distance_blk[None, None] == slash_group[:, :, None, None], axis=1)
        in_vert = jnp.any(key_block[None, None, :] == vert_group[:, :, None], axis=1)
        keep_blk = in_slash & (key_block >= 0)[None, None, :] & jnp.logical_not(in_vert)[:, None, :]
        whole_blk = keep_blk & (distance_blk != 0)[None]
        allow_diag = spread(whole_blk, BLOCK_TOKENS, BLOCK_TOKENS) | (
            spread(keep_blk & (distance_blk == 0)[None], BLOCK_TOKENS, BLOCK_TOKENS)
            & causal_ctx[None]
        )
        top_diag = jnp.max(jnp.where(allow_diag, score_diag, -jnp.inf), axis=2, keepdims=True)
        expo_diag = jnp.where(allow_diag, jnp.exp(score_diag - top_diag), 0.0)
        total_diag = jnp.sum(expo_diag, axis=2, keepdims=True)
        acc_diag = jnp.einsum(
            "htu,ud->htd",
            expo_diag.astype(jnp.bfloat16),
            context_v,
            preferred_element_type=jnp.float32,
        )

        arrived = arrived.reshape(2, cycle_size * capacity, BLOCK_TOKENS, head_dim)
        chosen = arrived[:, owner_dev * capacity + slot_index]
        vert_count = vert_group.shape[1]
        chosen = chosen.reshape(2, local_heads, vert_count * BLOCK_TOKENS, head_dim)
        vert_cols = jnp.repeat(vert_group, BLOCK_TOKENS, axis=1)
        row_block = jnp.repeat(query_block, BLOCK_TOKENS)
        causal_vert = jnp.tile(causal_tri, (block_count, vert_count))
        chunk_count = 2
        chunk_rows = token_count // chunk_count
        results = []
        for chunk in range(chunk_count):
            rows = slice(chunk * chunk_rows, (chunk + 1) * chunk_rows)
            q_part = query_heads[:, rows]
            score_vert = (
                jnp.einsum("htd,hud->htu", q_part, chosen[0], preferred_element_type=jnp.float32)
                * score_scale
            )
            blk_part = row_block[rows]
            allow_vert = (vert_cols[:, None, :] < blk_part[None, :, None]) | (
                (vert_cols[:, None, :] == blk_part[None, :, None]) & causal_vert[None, rows]
            )
            top_vert = jnp.max(jnp.where(allow_vert, score_vert, -jnp.inf), axis=2, keepdims=True)
            row_top = jnp.maximum(top_diag[:, rows], top_vert)
            expo_vert = jnp.where(allow_vert, jnp.exp(score_vert - row_top), 0.0)
            diag_scale = jnp.exp(top_diag[:, rows] - row_top)
            row_total = total_diag[:, rows] * diag_scale + jnp.sum(expo_vert, axis=2, keepdims=True)
            acc_vert = jnp.einsum(
                "htu,hud->htd",
                expo_vert.astype(jnp.bfloat16),
                chosen[1],
                preferred_element_type=jnp.float32,
            )
            head_out = (acc_diag[:, rows] * diag_scale + acc_vert) / row_total
            attention = head_out.astype(jnp.bfloat16).transpose(1, 0, 2).reshape(chunk_rows, -1)
            total = jnp.dot(attention, own_w, preferred_element_type=jnp.float32)
            for distance in range(1, heads_n):
                other = ring(attention, "heads", heads_n, distance)
                mine = lax.dynamic_slice_in_dim(other, core * half_rows, half_rows, 1)
                theirs = lax.dynamic_slice_in_dim(other, (1 - core) * half_rows, half_rows, 1)
                total = total + jnp.dot(
                    mine, fetched[distance - 1], preferred_element_type=jnp.float32
                )
                total = total + jnp.dot(
                    theirs, sibling_w[distance - 1], preferred_element_type=jnp.float32
                )
            results.append(total.astype(jnp.bfloat16))
        return jnp.concatenate(results, axis=0)

    return local


def split_mesh(mesh):
    devices = mesh.devices
    heads_n, seq_n = devices.shape
    core_n = 2
    y_n = len({d.coords[1] for d in devices.flat})
    z_n = seq_n // (core_n * y_n)
    sizes = (heads_n, z_n, y_n, core_n)
    return Mesh(np.asarray(devices).reshape(sizes), ("heads",) + SEQ), sizes


def solution(mesh):
    sub, sizes = split_mesh(mesh)
    return jax.shard_map(
        make_local(sizes),
        mesh=sub,
        in_specs=(
            P(SEQ, "heads"),
            P(SEQ, "heads"),
            P(SEQ, "heads"),
            P(),
            P(),
            P("heads", None),
        ),
        out_specs=P(SEQ, "heads"),
        check_vma=False,
    )
```

```python
import math

import jax
import jax.numpy as jnp
import functools

import numpy as np
from jax import lax
from jax.experimental import pallas as pl
from jax.sharding import Mesh
from jax.sharding import PartitionSpec as P

HEAD_SIZE = 128
BLOCK_TOKENS = 64
SEQ = ("z", "y", "core")


def shift(block, axis, size, distance):
    route = [(i, i + distance) for i in range(size) if 0 <= i + distance < size]
    return lax.ppermute(block, axis, route)


def ring(block, axis, size, distance):
    return lax.ppermute(block, axis, [(i, (i + distance) % size) for i in range(size)])


def spread(table, rows, cols):
    return jnp.repeat(jnp.repeat(table, rows, axis=-2), cols, axis=-1)


def vert_kernel(q_ref, k_ref, v_ref, cols_ref, rows_ref, top_ref, tot_ref, acc_ref, o_ref, *, scale):
    q = q_ref[0]
    k = k_ref[0]
    s = lax.dot_general(q, k, (((1,), (1,)), ((), ())), preferred_element_type=jnp.float32) * scale
    n_rows, n_cols = s.shape
    tpos = lax.broadcasted_iota(jnp.int32, (n_rows, n_cols), 0) & (BLOCK_TOKENS - 1)
    upos = lax.broadcasted_iota(jnp.int32, (n_rows, n_cols), 1) & (BLOCK_TOKENS - 1)
    vc = cols_ref[0]
    rb = rows_ref[...]
    allow = (vc < rb) | ((vc == rb) & (upos <= tpos))
    top_v = jnp.max(jnp.where(allow, s, -jnp.inf), axis=1, keepdims=True)
    top_d = top_ref[0]
    top = jnp.maximum(top_d, top_v)
    p = jnp.where(allow, jnp.exp(s - top), 0.0)
    sc = jnp.exp(top_d - top)
    total = tot_ref[0] * sc + jnp.sum(p, axis=1, keepdims=True)
    acc = jnp.dot(p.astype(jnp.bfloat16), v_ref[0], preferred_element_type=jnp.float32)
    o_ref[...] = ((acc_ref[0] * sc + acc) / total).astype(o_ref.dtype)


def vertical_attention(q, k, v, cols, rows, top_d, tot_d, acc_d, interpret=False):
    h, t, d = q.shape
    u = k.shape[1]
    kern = functools.partial(vert_kernel, scale=1.0 / math.sqrt(d))
    return pl.pallas_call(
        kern,
        grid=(h,),
        in_specs=[
            pl.BlockSpec((1, t, d), lambda i: (i, 0, 0)),
            pl.BlockSpec((1, u, d), lambda i: (i, 0, 0)),
            pl.BlockSpec((1, u, d), lambda i: (i, 0, 0)),
            pl.BlockSpec((1, 1, u), lambda i: (i, 0, 0)),
            pl.BlockSpec((t, 1), lambda i: (0, 0)),
            pl.BlockSpec((1, t, 1), lambda i: (i, 0, 0)),
            pl.BlockSpec((1, t, 1), lambda i: (i, 0, 0)),
            pl.BlockSpec((1, t, d), lambda i: (i, 0, 0)),
        ],
        out_specs=pl.BlockSpec((t, d), lambda i: (0, i)),
        out_shape=jax.ShapeDtypeStruct((t, h * d), jnp.bfloat16),
        interpret=interpret,
    )(q, k, v, cols, rows, top_d, tot_d, acc_d)


def make_local(sizes):
    heads_n, z_n, y_n, core_n = sizes
    cycle_size = z_n * y_n * core_n

    def local(queries, keys, values, vertical, slash, out_weight):
        head_dim = HEAD_SIZE
        local_heads = queries.shape[1] // head_dim
        token_count = queries.shape[0]
        block_count = token_count // BLOCK_TOKENS
        score_scale = 1.0 / math.sqrt(head_dim)
        kv_group = lax.axis_index("heads")
        core = lax.axis_index("core")
        cycle_index = lax.axis_index(SEQ)

        vert_group = lax.dynamic_slice_in_dim(vertical, kv_group * local_heads, local_heads, 0)
        slash_group = lax.dynamic_slice_in_dim(slash, kv_group * local_heads, local_heads, 0)
        union_list = vert_group.reshape(-1)
        listed_count = union_list.shape[0]
        owner_dev = union_list // block_count
        within_dev = union_list % block_count
        paired = jnp.stack([keys, values]).reshape(2, block_count, BLOCK_TOKENS, head_dim)
        owned_here = owner_dev == cycle_index
        capacity = min(block_count, max(2, 2 * listed_count // cycle_size))
        positions = jnp.arange(listed_count)
        same_owner = (owner_dev[:, None] == owner_dev[None, :]) & (
            positions[None, :] < positions[:, None]
        )
        slot_index = jnp.sum(same_owner.astype(jnp.int32), axis=1)
        selector = owned_here[None, :] & (slot_index[None, :] == jnp.arange(capacity)[:, None])
        picked = jnp.sum(jnp.where(selector, within_dev[None, :], 0), axis=1)
        outgoing = paired[:, picked].reshape(2, capacity * BLOCK_TOKENS, head_dim)
        arrived = lax.all_gather(outgoing, SEQ, axis=1, tiled=True)

        rows_total, width = out_weight.shape
        col_width = width // heads_n
        half_rows = rows_total // core_n
        fetched = []
        for distance in range(1, heads_n):
            dest_cols = ((kv_group + distance) % heads_n) * col_width
            piece = lax.dynamic_slice(out_weight, (core * half_rows, dest_cols), (half_rows, col_width))
            fetched.append(ring(piece, "heads", heads_n, distance))
        fetched = jnp.stack(fetched)
        sibling_w = ring(fetched, "core", core_n, 1)
        own_w = lax.dynamic_slice(out_weight, (0, kv_group * col_width), (rows_total, col_width))

        earlier = shift(paired, SEQ, cycle_size, 1)
        farther = shift(paired, SEQ, cycle_size, 2)
        context = jnp.concatenate([farther, earlier, paired], axis=1)
        context_blocks = context.shape[1]
        context_k = context[0].reshape(context_blocks * BLOCK_TOKENS, head_dim)
        context_v = context[1].reshape(context_blocks * BLOCK_TOKENS, head_dim)
        first_block = cycle_index * block_count
        query_block = first_block + jnp.arange(block_count, dtype=jnp.int32)
        key_block = first_block - (context_blocks - block_count) + jnp.arange(
            context_blocks, dtype=jnp.int32
        )
        distance_blk = query_block[:, None] - key_block[None, :]
        token_pos = jnp.arange(BLOCK_TOKENS)
        causal_tri = token_pos[None, :] <= token_pos[:, None]
        causal_ctx = jnp.tile(causal_tri, (block_count, context_blocks))

        query_heads = queries.reshape(token_count, local_heads, head_dim).transpose(1, 0, 2)
        score_diag = (
            jnp.einsum("htd,ud->htu", query_heads, context_k, preferred_element_type=jnp.float32)
            * score_scale
        )
        in_slash = jnp.any(distance_blk[None, None] == slash_group[:, :, None, None], axis=1)
        in_vert = jnp.any(key_block[None, None, :] == vert_group[:, :, None], axis=1)
        keep_blk = in_slash & (key_block >= 0)[None, None, :] & jnp.logical_not(in_vert)[:, None, :]
        whole_blk = keep_blk & (distance_blk != 0)[None]
        allow_diag = spread(whole_blk, BLOCK_TOKENS, BLOCK_TOKENS) | (
            spread(keep_blk & (distance_blk == 0)[None], BLOCK_TOKENS, BLOCK_TOKENS)
            & causal_ctx[None]
        )
        top_diag = jnp.max(jnp.where(allow_diag, score_diag, -jnp.inf), axis=2, keepdims=True)
        expo_diag = jnp.where(allow_diag, jnp.exp(score_diag - top_diag), 0.0)
        total_diag = jnp.sum(expo_diag, axis=2, keepdims=True)
        acc_diag = jnp.einsum(
            "htu,ud->htd",
            expo_diag.astype(jnp.bfloat16),
            context_v,
            preferred_element_type=jnp.float32,
        )

        arrived = arrived.reshape(2, cycle_size * capacity, BLOCK_TOKENS, head_dim)
        chosen = arrived[:, owner_dev * capacity + slot_index]
        vert_count = vert_group.shape[1]
        chosen = chosen.reshape(2, local_heads, vert_count * BLOCK_TOKENS, head_dim)
        vert_cols = jnp.repeat(vert_group, BLOCK_TOKENS, axis=1)[:, None, :]
        row_block = jnp.repeat(query_block, BLOCK_TOKENS)[:, None]
        attention = vertical_attention(
            query_heads, chosen[0], chosen[1], vert_cols, row_block, top_diag, total_diag, acc_diag
        )

        weight_stack = [own_w]
        for distance in range(1, heads_n):
            weight_stack += [fetched[distance - 1], sibling_w[distance - 1]]
        weight_stack = jnp.concatenate(weight_stack, axis=0)
        attention_stack = [attention]
        for distance in range(1, heads_n):
            other = ring(attention, "heads", heads_n, distance)
            attention_stack.append(lax.dynamic_slice_in_dim(other, core * half_rows, half_rows, 1))
            attention_stack.append(
                lax.dynamic_slice_in_dim(other, (1 - core) * half_rows, half_rows, 1)
            )
        attention_stack = jnp.concatenate(attention_stack, axis=1)
        total = jnp.dot(attention_stack, weight_stack, preferred_element_type=jnp.float32)
        return total.astype(jnp.bfloat16)

    return local


def split_mesh(mesh):
    devices = mesh.devices
    heads_n, seq_n = devices.shape
    core_n = 2
    y_n = len({d.coords[1] for d in devices.flat})
    z_n = seq_n // (core_n * y_n)
    sizes = (heads_n, z_n, y_n, core_n)
    return Mesh(np.asarray(devices).reshape(sizes), ("heads",) + SEQ), sizes


def solution(mesh):
    sub, sizes = split_mesh(mesh)
    return jax.shard_map(
        make_local(sizes),
        mesh=sub,
        in_specs=(
            P(SEQ, "heads"),
            P(SEQ, "heads"),
            P(SEQ, "heads"),
            P(),
            P(),
            P("heads", None),
        ),
        out_specs=P(SEQ, "heads"),
        check_vma=False,
    )
```

```python
import math

import jax
import jax.numpy as jnp
import functools

import numpy as np
from jax import lax
from jax.experimental import pallas as pl
from jax.sharding import Mesh
from jax.sharding import PartitionSpec as P

HEAD_SIZE = 128
BLOCK_TOKENS = 64
SEQ = ("z", "y", "core")


def shift(block, axis, size, distance):
    route = [(i, i + distance) for i in range(size) if 0 <= i + distance < size]
    return lax.ppermute(block, axis, route)


def ring(block, axis, size, distance):
    return lax.ppermute(block, axis, [(i, (i + distance) % size) for i in range(size)])


def spread(table, rows, cols):
    return jnp.repeat(jnp.repeat(table, rows, axis=-2), cols, axis=-1)


def vert_kernel(q_ref, k_ref, v_ref, cols_ref, rows_ref, top_ref, tot_ref, acc_ref, o_ref, *, scale):
    q = q_ref[0]
    k = k_ref[0]
    s = lax.dot_general(q, k, (((1,), (1,)), ((), ())), preferred_element_type=jnp.float32) * scale
    n_rows, n_cols = s.shape
    tpos = lax.broadcasted_iota(jnp.int32, (n_rows, n_cols), 0) & (BLOCK_TOKENS - 1)
    upos = lax.broadcasted_iota(jnp.int32, (n_rows, n_cols), 1) & (BLOCK_TOKENS - 1)
    vc = cols_ref[0]
    rb = rows_ref[...]
    allow = (vc < rb) | ((vc == rb) & (upos <= tpos))
    top_v = jnp.max(jnp.where(allow, s, -jnp.inf), axis=1, keepdims=True)
    top_d = top_ref[0]
    top = jnp.maximum(top_d, top_v)
    p = jnp.where(allow, jnp.exp(s - top), 0.0)
    sc = jnp.exp(top_d - top)
    total = tot_ref[0] * sc + jnp.sum(p, axis=1, keepdims=True)
    acc = jnp.dot(p.astype(jnp.bfloat16), v_ref[0], preferred_element_type=jnp.float32)
    o_ref[...] = ((acc_ref[0] * sc + acc) / total).astype(o_ref.dtype)


def vertical_attention(q, k, v, cols, rows, top_d, tot_d, acc_d, interpret=False):
    h, t, d = q.shape
    u = k.shape[1]
    kern = functools.partial(vert_kernel, scale=1.0 / math.sqrt(d))
    return pl.pallas_call(
        kern,
        grid=(h,),
        in_specs=[
            pl.BlockSpec((1, t, d), lambda i: (i, 0, 0)),
            pl.BlockSpec((1, u, d), lambda i: (i, 0, 0)),
            pl.BlockSpec((1, u, d), lambda i: (i, 0, 0)),
            pl.BlockSpec((1, 1, u), lambda i: (i, 0, 0)),
            pl.BlockSpec((t, 1), lambda i: (0, 0)),
            pl.BlockSpec((1, t, 1), lambda i: (i, 0, 0)),
            pl.BlockSpec((1, t, 1), lambda i: (i, 0, 0)),
            pl.BlockSpec((1, t, d), lambda i: (i, 0, 0)),
        ],
        out_specs=pl.BlockSpec((t, d), lambda i: (0, i)),
        out_shape=jax.ShapeDtypeStruct((t, h * d), jnp.bfloat16),
        interpret=interpret,
    )(q, k, v, cols, rows, top_d, tot_d, acc_d)


def make_local(sizes):
    heads_n, z_n, y_n, core_n = sizes
    cycle_size = z_n * y_n * core_n

    def local(queries, keys, values, vertical, slash, out_weight):
        head_dim = HEAD_SIZE
        local_heads = queries.shape[1] // head_dim
        token_count = queries.shape[0]
        block_count = token_count // BLOCK_TOKENS
        score_scale = 1.0 / math.sqrt(head_dim)
        kv_group = lax.axis_index("heads")
        core = lax.axis_index("core")
        cycle_index = lax.axis_index(SEQ)

        vert_group = lax.dynamic_slice_in_dim(vertical, kv_group * local_heads, local_heads, 0)
        slash_group = lax.dynamic_slice_in_dim(slash, kv_group * local_heads, local_heads, 0)
        union_list = vert_group.reshape(-1)
        listed_count = union_list.shape[0]
        owner_dev = union_list // block_count
        within_dev = union_list % block_count
        paired = jnp.stack([keys, values]).reshape(2, block_count, BLOCK_TOKENS, head_dim)
        owned_here = owner_dev == cycle_index
        capacity = 2
        low = jnp.min(jnp.where(owned_here, within_dev, block_count - 1))
        high = jnp.max(jnp.where(owned_here, within_dev, 0))
        outgoing = jnp.concatenate(
            [
                lax.dynamic_slice_in_dim(paired, low, 1, 1),
                lax.dynamic_slice_in_dim(paired, high, 1, 1),
            ],
            axis=1,
        ).reshape(2, capacity * BLOCK_TOKENS, head_dim)
        same_owner = (owner_dev[:, None] == owner_dev[None, :]) & (
            union_list[None, :] < union_list[:, None]
        )
        slot_index = jnp.sum(same_owner.astype(jnp.int32), axis=1)
        arrived = lax.all_gather(outgoing, SEQ, axis=1, tiled=True)

        rows_total, width = out_weight.shape
        col_width = width // heads_n
        half_rows = rows_total // core_n
        fetched = []
        for distance in range(1, heads_n):
            dest_cols = ((kv_group + distance) % heads_n) * col_width
            piece = lax.dynamic_slice(out_weight, (core * half_rows, dest_cols), (half_rows, col_width))
            fetched.append(ring(piece, "heads", heads_n, distance))
        fetched = jnp.stack(fetched)
        sibling_w = ring(fetched, "core", core_n, 1)
        own_w = lax.dynamic_slice(out_weight, (0, kv_group * col_width), (rows_total, col_width))

        earlier = shift(paired, SEQ, cycle_size, 1)
        farther = shift(paired, SEQ, cycle_size, 2)
        context = jnp.concatenate([farther, earlier, paired], axis=1)
        context_blocks = context.shape[1]
        context_k = context[0].reshape(context_blocks * BLOCK_TOKENS, head_dim)
        context_v = context[1].reshape(context_blocks * BLOCK_TOKENS, head_dim)
        first_block = cycle_index * block_count
        query_block = first_block + jnp.arange(block_count, dtype=jnp.int32)
        key_block = first_block - (context_blocks - block_count) + jnp.arange(
            context_blocks, dtype=jnp.int32
        )
        distance_blk = query_block[:, None] - key_block[None, :]
        token_pos = jnp.arange(BLOCK_TOKENS)
        causal_tri = token_pos[None, :] <= token_pos[:, None]
        causal_ctx = jnp.tile(causal_tri, (block_count, context_blocks))

        query_heads = queries.reshape(token_count, local_heads, head_dim).transpose(1, 0, 2)
        score_diag = (
            jnp.einsum("htd,ud->htu", query_heads, context_k, preferred_element_type=jnp.float32)
            * score_scale
        )
        in_slash = jnp.any(distance_blk[None, None] == slash_group[:, :, None, None], axis=1)
        in_vert = jnp.any(key_block[None, None, :] == vert_group[:, :, None], axis=1)
        keep_blk = in_slash & (key_block >= 0)[None, None, :] & jnp.logical_not(in_vert)[:, None, :]
        whole_blk = keep_blk & (distance_blk != 0)[None]
        allow_diag = spread(whole_blk, BLOCK_TOKENS, BLOCK_TOKENS) | (
            spread(keep_blk & (distance_blk == 0)[None], BLOCK_TOKENS, BLOCK_TOKENS)
            & causal_ctx[None]
        )
        top_diag = jnp.max(jnp.where(allow_diag, score_diag, -jnp.inf), axis=2, keepdims=True)
        expo_diag = jnp.where(allow_diag, jnp.exp(score_diag - top_diag), 0.0)
        total_diag = jnp.sum(expo_diag, axis=2, keepdims=True)
        acc_diag = jnp.einsum(
            "htu,ud->htd",
            expo_diag.astype(jnp.bfloat16),
            context_v,
            preferred_element_type=jnp.float32,
        )

        arrived = arrived.reshape(2, cycle_size * capacity, BLOCK_TOKENS, head_dim)
        chosen = arrived[:, owner_dev * capacity + slot_index]
        vert_count = vert_group.shape[1]
        chosen = chosen.reshape(2, local_heads, vert_count * BLOCK_TOKENS, head_dim)
        vert_cols = jnp.repeat(vert_group, BLOCK_TOKENS, axis=1)[:, None, :]
        row_block = jnp.repeat(query_block, BLOCK_TOKENS)[:, None]
        attention = vertical_attention(
            query_heads, chosen[0], chosen[1], vert_cols, row_block, top_diag, total_diag, acc_diag
        )

        def rows_of(distance):
            mine, theirs = fetched[distance - 1], sibling_w[distance - 1]
            return jnp.where(
                core == 0,
                jnp.concatenate([mine, theirs], axis=0),
                jnp.concatenate([theirs, mine], axis=0),
            )

        half_cols = attention.shape[1] // 2
        behind = ring(attention, "heads", heads_n, 1)
        ahead = ring(attention, "heads", heads_n, heads_n - 1)
        total = jnp.dot(attention, own_w, preferred_element_type=jnp.float32)
        far_low = ring(behind[:, :half_cols], "heads", heads_n, 1)
        far_high = ring(ahead[:, half_cols:], "heads", heads_n, heads_n - 1)
        total = total + jnp.dot(behind, rows_of(1), preferred_element_type=jnp.float32)
        total = total + jnp.dot(ahead, rows_of(heads_n - 1), preferred_element_type=jnp.float32)
        far = jnp.concatenate([far_low, far_high], axis=1)
        total = total + jnp.dot(far, rows_of(2), preferred_element_type=jnp.float32)
        return total.astype(jnp.bfloat16)

    return local


def split_mesh(mesh):
    devices = mesh.devices
    heads_n, seq_n = devices.shape
    core_n = 2
    y_n = len({d.coords[1] for d in devices.flat})
    z_n = seq_n // (core_n * y_n)
    sizes = (heads_n, z_n, y_n, core_n)
    return Mesh(np.asarray(devices).reshape(sizes), ("heads",) + SEQ), sizes


def solution(mesh):
    sub, sizes = split_mesh(mesh)
    return jax.shard_map(
        make_local(sizes),
        mesh=sub,
        in_specs=(
            P(SEQ, "heads"),
            P(SEQ, "heads"),
            P(SEQ, "heads"),
            P(),
            P(),
            P("heads", None),
        ),
        out_specs=P(SEQ, "heads"),
        check_vma=False,
    )
```

```python
import math

import jax
import jax.numpy as jnp
import functools

import numpy as np
from jax import lax
from jax.experimental import pallas as pl
from jax.experimental.pallas import tpu as pltpu
from jax.sharding import Mesh
from jax.sharding import PartitionSpec as P

HEAD_SIZE = 128
BLOCK_TOKENS = 64
SEQ = ("z", "y", "core")


def shift(block, axis, size, distance):
    route = [(i, i + distance) for i in range(size) if 0 <= i + distance < size]
    return lax.ppermute(block, axis, route)


def ring(block, axis, size, distance):
    return lax.ppermute(block, axis, [(i, (i + distance) % size) for i in range(size)])


def spread(table, rows, cols):
    return jnp.repeat(jnp.repeat(table, rows, axis=-2), cols, axis=-1)


def vertical_kernel(slots_ref, q_ref, kv_hbm, key_tok_ref, query_tok_ref, top_ref, tot_ref, acc_ref,
                    o_ref, k_buf, v_buf, sems, *, scale):
    head = pl.program_id(0)
    vert_count = k_buf.shape[0] // BLOCK_TOKENS
    copies = []
    for n in range(vert_count):
        slot = slots_ref[head, n]
        rows = pl.ds(n * BLOCK_TOKENS, BLOCK_TOKENS)
        for part, buf in ((0, k_buf), (1, v_buf)):
            copy = pltpu.make_async_copy(kv_hbm.at[part, slot], buf.at[rows], sems.at[part, n])
            copy.start()
            copies.append(copy)
    for copy in copies:
        copy.wait()
    s = lax.dot_general(
        q_ref[0], k_buf[...], (((1,), (1,)), ((), ())), preferred_element_type=jnp.float32
    ) * scale
    s = jnp.where(key_tok_ref[0] <= query_tok_ref[...], s, -jnp.inf)
    top_d = top_ref[0]
    top = jnp.maximum(top_d, jnp.max(s, axis=1, keepdims=True))
    p = jnp.exp(s - top)
    sc = jnp.exp(top_d - top)
    total = tot_ref[0] * sc + jnp.sum(p, axis=1, keepdims=True)
    acc = jnp.dot(p.astype(jnp.bfloat16), v_buf[...], preferred_element_type=jnp.float32)
    o_ref[...] = ((acc_ref[0] * sc + acc) / total).astype(o_ref.dtype)


def vertical_attention(slots, q, kv, key_tok, query_tok, top_d, tot_d, acc_d, interpret=False):
    heads, rows, dim = q.shape
    keys_n = key_tok.shape[-1]
    kernel = functools.partial(vertical_kernel, scale=1.0 / math.sqrt(dim))
    grid_spec = pltpu.PrefetchScalarGridSpec(
        num_scalar_prefetch=1,
        grid=(heads,),
        in_specs=[
            pl.BlockSpec((1, rows, dim), lambda i, t: (i, 0, 0)),
            pl.BlockSpec(memory_space=pl.ANY),
            pl.BlockSpec((1, 1, keys_n), lambda i, t: (i, 0, 0)),
            pl.BlockSpec((rows, 1), lambda i, t: (0, 0)),
            pl.BlockSpec((1, rows, 1), lambda i, t: (i, 0, 0)),
            pl.BlockSpec((1, rows, 1), lambda i, t: (i, 0, 0)),
            pl.BlockSpec((1, rows, dim), lambda i, t: (i, 0, 0)),
        ],
        out_specs=pl.BlockSpec((rows, dim), lambda i, t: (0, i)),
        scratch_shapes=[
            pltpu.VMEM((keys_n, dim), kv.dtype),
            pltpu.VMEM((keys_n, dim), kv.dtype),
            pltpu.SemaphoreType.DMA((2, keys_n // BLOCK_TOKENS)),
        ],
    )
    return pl.pallas_call(
        kernel,
        grid_spec=grid_spec,
        out_shape=jax.ShapeDtypeStruct((rows, heads * dim), jnp.bfloat16),
        interpret=interpret,
    )(slots, q, kv, key_tok, query_tok, top_d, tot_d, acc_d)


def make_local(sizes):
    heads_n, z_n, y_n, core_n = sizes
    cycle_size = z_n * y_n * core_n

    def local(queries, keys, values, vertical, slash, out_weight):
        head_dim = HEAD_SIZE
        local_heads = queries.shape[1] // head_dim
        token_count = queries.shape[0]
        block_count = token_count // BLOCK_TOKENS
        score_scale = 1.0 / math.sqrt(head_dim)
        kv_group = lax.axis_index("heads")
        core = lax.axis_index("core")
        cycle_index = lax.axis_index(SEQ)

        vert_group = lax.dynamic_slice_in_dim(vertical, kv_group * local_heads, local_heads, 0)
        slash_group = lax.dynamic_slice_in_dim(slash, kv_group * local_heads, local_heads, 0)
        union_list = vert_group.reshape(-1)
        listed_count = union_list.shape[0]
        owner_dev = union_list // block_count
        within_dev = union_list % block_count
        paired = jnp.stack([keys, values]).reshape(2, block_count, BLOCK_TOKENS, head_dim)
        owned_here = owner_dev == cycle_index
        capacity = 2
        low = jnp.min(jnp.where(owned_here, within_dev, block_count - 1))
        high = jnp.max(jnp.where(owned_here, within_dev, 0))
        outgoing = jnp.concatenate(
            [
                lax.dynamic_slice_in_dim(paired, low, 1, 1),
                lax.dynamic_slice_in_dim(paired, high, 1, 1),
            ],
            axis=1,
        ).reshape(2, capacity * BLOCK_TOKENS, head_dim)
        same_owner = (owner_dev[:, None] == owner_dev[None, :]) & (
            union_list[None, :] < union_list[:, None]
        )
        slot_index = jnp.sum(same_owner.astype(jnp.int32), axis=1)
        arrived = lax.all_gather(outgoing, SEQ, axis=1, tiled=True)

        rows_total, width = out_weight.shape
        col_width = width // heads_n
        half_rows = rows_total // core_n
        fetched = []
        for distance in range(1, heads_n):
            dest_cols = ((kv_group + distance) % heads_n) * col_width
            piece = lax.dynamic_slice(out_weight, (core * half_rows, dest_cols), (half_rows, col_width))
            fetched.append(ring(piece, "heads", heads_n, distance))
        fetched = jnp.stack(fetched)
        sibling_w = ring(fetched, "core", core_n, 1)
        own_w = lax.dynamic_slice(out_weight, (0, kv_group * col_width), (rows_total, col_width))

        earlier = shift(paired, SEQ, cycle_size, 1)
        farther = shift(paired, SEQ, cycle_size, 2)
        context = jnp.concatenate([farther, earlier, paired], axis=1)
        context_blocks = context.shape[1]
        context_k = context[0].reshape(context_blocks * BLOCK_TOKENS, head_dim)
        context_v = context[1].reshape(context_blocks * BLOCK_TOKENS, head_dim)
        first_block = cycle_index * block_count
        query_block = first_block + jnp.arange(block_count, dtype=jnp.int32)
        key_block = first_block - (context_blocks - block_count) + jnp.arange(
            context_blocks, dtype=jnp.int32
        )
        distance_blk = query_block[:, None] - key_block[None, :]
        token_pos = jnp.arange(BLOCK_TOKENS)
        causal_tri = token_pos[None, :] <= token_pos[:, None]
        causal_ctx = jnp.tile(causal_tri, (block_count, context_blocks))

        query_heads = queries.reshape(token_count, local_heads, head_dim).transpose(1, 0, 2)
        score_diag = (
            jnp.einsum("htd,ud->htu", query_heads, context_k, preferred_element_type=jnp.float32)
            * score_scale
        )
        in_slash = jnp.any(distance_blk[None, None] == slash_group[:, :, None, None], axis=1)
        in_vert = jnp.any(key_block[None, None, :] == vert_group[:, :, None], axis=1)
        keep_blk = in_slash & (key_block >= 0)[None, None, :] & jnp.logical_not(in_vert)[:, None, :]
        whole_blk = keep_blk & (distance_blk != 0)[None]
        allow_diag = spread(whole_blk, BLOCK_TOKENS, BLOCK_TOKENS) | (
            spread(keep_blk & (distance_blk == 0)[None], BLOCK_TOKENS, BLOCK_TOKENS)
            & causal_ctx[None]
        )
        top_diag = jnp.max(jnp.where(allow_diag, score_diag, -jnp.inf), axis=2, keepdims=True)
        expo_diag = jnp.where(allow_diag, jnp.exp(score_diag - top_diag), 0.0)
        total_diag = jnp.sum(expo_diag, axis=2, keepdims=True)
        acc_diag = jnp.einsum(
            "htu,ud->htd",
            expo_diag.astype(jnp.bfloat16),
            context_v,
            preferred_element_type=jnp.float32,
        )

        arrived = arrived.reshape(2, cycle_size * capacity, BLOCK_TOKENS, head_dim)
        vert_count = vert_group.shape[1]
        slots = (owner_dev * capacity + slot_index).reshape(local_heads, vert_count)
        key_tok = (vert_group[:, :, None] * BLOCK_TOKENS + token_pos).reshape(local_heads, 1, -1)
        query_tok = (first_block * BLOCK_TOKENS + jnp.arange(token_count, dtype=jnp.int32))[:, None]
        attention = vertical_attention(
            slots.astype(jnp.int32),
            query_heads,
            arrived,
            key_tok.astype(jnp.int32),
            query_tok,
            top_diag,
            total_diag,
            acc_diag,
        )

        def rows_of(distance):
            mine, theirs = fetched[distance - 1], sibling_w[distance - 1]
            return jnp.where(
                core == 0,
                jnp.concatenate([mine, theirs], axis=0),
                jnp.concatenate([theirs, mine], axis=0),
            )

        half_cols = attention.shape[1] // 2
        behind = ring(attention, "heads", heads_n, 1)
        ahead = ring(attention, "heads", heads_n, heads_n - 1)
        total = jnp.dot(attention, own_w, preferred_element_type=jnp.float32)
        far_low = ring(behind[:, :half_cols], "heads", heads_n, 1)
        far_high = ring(ahead[:, half_cols:], "heads", heads_n, heads_n - 1)
        total = total + jnp.dot(behind, rows_of(1), preferred_element_type=jnp.float32)
        total = total + jnp.dot(ahead, rows_of(heads_n - 1), preferred_element_type=jnp.float32)
        far = jnp.concatenate([far_low, far_high], axis=1)
        total = total + jnp.dot(far, rows_of(2), preferred_element_type=jnp.float32)
        return total.astype(jnp.bfloat16)

    return local


def split_mesh(mesh):
    devices = mesh.devices
    heads_n, seq_n = devices.shape
    core_n = 2
    y_n = len({d.coords[1] for d in devices.flat})
    z_n = seq_n // (core_n * y_n)
    sizes = (heads_n, z_n, y_n, core_n)
    return Mesh(np.asarray(devices).reshape(sizes), ("heads",) + SEQ), sizes


def solution(mesh):
    sub, sizes = split_mesh(mesh)
    return jax.shard_map(
        make_local(sizes),
        mesh=sub,
        in_specs=(
            P(SEQ, "heads"),
            P(SEQ, "heads"),
            P(SEQ, "heads"),
            P(),
            P(),
            P("heads", None),
        ),
        out_specs=P(SEQ, "heads"),
        check_vma=False,
    )
```

```python
import math

import jax
import jax.numpy as jnp
import functools

import numpy as np
from jax import lax
from jax.experimental import pallas as pl
from jax.experimental.pallas import tpu as pltpu
from jax.sharding import Mesh
from jax.sharding import PartitionSpec as P

HEAD_SIZE = 128
BLOCK_TOKENS = 64
SEQ = ("z", "y", "core")


def shift(block, axis, size, distance):
    route = [(i, i + distance) for i in range(size) if 0 <= i + distance < size]
    return lax.ppermute(block, axis, route)


def ring(block, axis, size, distance):
    return lax.ppermute(block, axis, [(i, (i + distance) % size) for i in range(size)])


def spread(table, rows, cols):
    return jnp.repeat(jnp.repeat(table, rows, axis=-2), cols, axis=-1)


def vertical_kernel(slots_ref, q_ref, kv_hbm, key_tok_ref, query_tok_ref, top_ref, tot_ref, acc_ref,
                    o_ref, k_buf, v_buf, sems, *, scale):
    head = pl.program_id(0)
    heads = pl.num_programs(0)
    vert_count = k_buf.shape[1] // BLOCK_TOKENS

    def block_copies(h, buf_index):
        copies = []
        for n in range(vert_count):
            slot = slots_ref[h, n]
            rows = pl.ds(n * BLOCK_TOKENS, BLOCK_TOKENS)
            for part, buf in ((0, k_buf), (1, v_buf)):
                copies.append(
                    pltpu.make_async_copy(
                        kv_hbm.at[part, slot], buf.at[buf_index, rows], sems.at[buf_index, part, n]
                    )
                )
        return copies

    current = head % 2

    @pl.when(head == 0)
    def _():
        for copy in block_copies(0, 0):
            copy.start()

    @pl.when(head + 1 < heads)
    def _():
        for copy in block_copies(head + 1, 1 - current):
            copy.start()

    for copy in block_copies(head, current):
        copy.wait()
    s = lax.dot_general(
        q_ref[0], k_buf[current], (((1,), (1,)), ((), ())), preferred_element_type=jnp.float32
    ) * scale
    s = jnp.where(key_tok_ref[0] <= query_tok_ref[...], s, -jnp.inf)
    top_d = top_ref[0]
    top = jnp.maximum(top_d, jnp.max(s, axis=1, keepdims=True))
    p = jnp.exp(s - top)
    sc = jnp.exp(top_d - top)
    total = tot_ref[0] * sc + jnp.sum(p, axis=1, keepdims=True)
    acc = jnp.dot(p.astype(jnp.bfloat16), v_buf[current], preferred_element_type=jnp.float32)
    o_ref[...] = ((acc_ref[0] * sc + acc) / total).astype(o_ref.dtype)


def vertical_attention(slots, q, kv, key_tok, query_tok, top_d, tot_d, acc_d, interpret=False):
    heads, rows, dim = q.shape
    keys_n = key_tok.shape[-1]
    kernel = functools.partial(vertical_kernel, scale=1.0 / math.sqrt(dim))
    grid_spec = pltpu.PrefetchScalarGridSpec(
        num_scalar_prefetch=1,
        grid=(heads,),
        in_specs=[
            pl.BlockSpec((1, rows, dim), lambda i, t: (i, 0, 0)),
            pl.BlockSpec(memory_space=pl.ANY),
            pl.BlockSpec((1, 1, keys_n), lambda i, t: (i, 0, 0)),
            pl.BlockSpec((rows, 1), lambda i, t: (0, 0)),
            pl.BlockSpec((1, rows, 1), lambda i, t: (i, 0, 0)),
            pl.BlockSpec((1, rows, 1), lambda i, t: (i, 0, 0)),
            pl.BlockSpec((1, rows, dim), lambda i, t: (i, 0, 0)),
        ],
        out_specs=pl.BlockSpec((rows, dim), lambda i, t: (0, i)),
        scratch_shapes=[
            pltpu.VMEM((2, keys_n, dim), kv.dtype),
            pltpu.VMEM((2, keys_n, dim), kv.dtype),
            pltpu.SemaphoreType.DMA((2, 2, keys_n // BLOCK_TOKENS)),
        ],
    )
    return pl.pallas_call(
        kernel,
        grid_spec=grid_spec,
        out_shape=jax.ShapeDtypeStruct((rows, heads * dim), jnp.bfloat16),
        interpret=interpret,
    )(slots, q, kv, key_tok, query_tok, top_d, tot_d, acc_d)


def make_local(sizes):
    heads_n, z_n, y_n, core_n = sizes
    cycle_size = z_n * y_n * core_n

    def local(queries, keys, values, vertical, slash, out_weight):
        head_dim = HEAD_SIZE
        local_heads = queries.shape[1] // head_dim
        token_count = queries.shape[0]
        block_count = token_count // BLOCK_TOKENS
        score_scale = 1.0 / math.sqrt(head_dim)
        kv_group = lax.axis_index("heads")
        core = lax.axis_index("core")
        cycle_index = lax.axis_index(SEQ)

        vert_group = lax.dynamic_slice_in_dim(vertical, kv_group * local_heads, local_heads, 0)
        slash_group = lax.dynamic_slice_in_dim(slash, kv_group * local_heads, local_heads, 0)
        union_list = vert_group.reshape(-1)
        listed_count = union_list.shape[0]
        owner_dev = union_list // block_count
        within_dev = union_list % block_count
        paired = jnp.stack([keys, values]).reshape(2, block_count, BLOCK_TOKENS, head_dim)
        owned_here = owner_dev == cycle_index
        capacity = 2
        local_ids = jnp.arange(block_count, dtype=jnp.int32)
        owned_blocks = jnp.any(
            owned_here[None, :] & (within_dev[None, :] == local_ids[:, None]), axis=1
        )
        below = jnp.sum(
            (owned_blocks[None, :] & (local_ids[None, :] < local_ids[:, None])).astype(jnp.int32),
            axis=1,
        )
        owned_total = jnp.sum(owned_blocks.astype(jnp.int32))
        pick = jnp.stack(
            [owned_blocks & (below == 0), owned_blocks & (below == owned_total - 1)]
        ).astype(jnp.bfloat16)
        outgoing = jnp.einsum(
            "cb,kbtd->kctd", pick, paired, preferred_element_type=jnp.float32
        ).astype(jnp.bfloat16).reshape(2, capacity * BLOCK_TOKENS, head_dim)
        same_owner = (owner_dev[:, None] == owner_dev[None, :]) & (
            union_list[None, :] < union_list[:, None]
        )
        slot_index = jnp.sum(same_owner.astype(jnp.int32), axis=1)
        arrived = lax.all_gather(outgoing, SEQ, axis=1, tiled=True)

        rows_total, width = out_weight.shape
        col_width = width // heads_n
        half_rows = rows_total // core_n
        fetched = []
        for distance in range(1, heads_n):
            dest_cols = ((kv_group + distance) % heads_n) * col_width
            piece = lax.dynamic_slice(out_weight, (core * half_rows, dest_cols), (half_rows, col_width))
            fetched.append(ring(piece, "heads", heads_n, distance))
        fetched = jnp.stack(fetched)
        sibling_w = ring(fetched, "core", core_n, 1)
        own_w = lax.dynamic_slice(out_weight, (0, kv_group * col_width), (rows_total, col_width))

        earlier = shift(paired, SEQ, cycle_size, 1)
        farther = shift(paired, SEQ, cycle_size, 2)
        context = jnp.concatenate([farther, earlier, paired], axis=1)
        context_blocks = context.shape[1]
        context_k = context[0].reshape(context_blocks * BLOCK_TOKENS, head_dim)
        context_v = context[1].reshape(context_blocks * BLOCK_TOKENS, head_dim)
        first_block = cycle_index * block_count
        query_block = first_block + jnp.arange(block_count, dtype=jnp.int32)
        key_block = first_block - (context_blocks - block_count) + jnp.arange(
            context_blocks, dtype=jnp.int32
        )
        distance_blk = query_block[:, None] - key_block[None, :]
        token_pos = jnp.arange(BLOCK_TOKENS)
        causal_tri = token_pos[None, :] <= token_pos[:, None]
        causal_ctx = jnp.tile(causal_tri, (block_count, context_blocks))

        query_heads = queries.reshape(token_count, local_heads, head_dim).transpose(1, 0, 2)
        score_diag = (
            jnp.einsum("htd,ud->htu", query_heads, context_k, preferred_element_type=jnp.float32)
            * score_scale
        )
        in_slash = jnp.any(distance_blk[None, None] == slash_group[:, :, None, None], axis=1)
        in_vert = jnp.any(key_block[None, None, :] == vert_group[:, :, None], axis=1)
        keep_blk = in_slash & (key_block >= 0)[None, None, :] & jnp.logical_not(in_vert)[:, None, :]
        whole_blk = keep_blk & (distance_blk != 0)[None]
        allow_diag = spread(whole_blk, BLOCK_TOKENS, BLOCK_TOKENS) | (
            spread(keep_blk & (distance_blk == 0)[None], BLOCK_TOKENS, BLOCK_TOKENS)
            & causal_ctx[None]
        )
        top_diag = jnp.max(jnp.where(allow_diag, score_diag, -jnp.inf), axis=2, keepdims=True)
        expo_diag = jnp.where(allow_diag, jnp.exp(score_diag - top_diag), 0.0)
        total_diag = jnp.sum(expo_diag, axis=2, keepdims=True)
        acc_diag = jnp.einsum(
            "htu,ud->htd",
            expo_diag.astype(jnp.bfloat16),
            context_v,
            preferred_element_type=jnp.float32,
        )

        arrived = arrived.reshape(2, cycle_size * capacity, BLOCK_TOKENS, head_dim)
        vert_count = vert_group.shape[1]
        slots = (owner_dev * capacity + slot_index).reshape(local_heads, vert_count)
        key_tok = (vert_group[:, :, None] * BLOCK_TOKENS + token_pos).reshape(local_heads, 1, -1)
        query_tok = (first_block * BLOCK_TOKENS + jnp.arange(token_count, dtype=jnp.int32))[:, None]
        attention = vertical_attention(
            slots.astype(jnp.int32),
            query_heads,
            arrived,
            key_tok.astype(jnp.int32),
            query_tok,
            top_diag,
            total_diag,
            acc_diag,
        )

        def rows_of(distance):
            mine, theirs = fetched[distance - 1], sibling_w[distance - 1]
            return jnp.where(
                core == 0,
                jnp.concatenate([mine, theirs], axis=0),
                jnp.concatenate([theirs, mine], axis=0),
            )

        half_cols = attention.shape[1] // 2
        behind = ring(attention, "heads", heads_n, 1)
        ahead = ring(attention, "heads", heads_n, heads_n - 1)
        total = jnp.dot(attention, own_w, preferred_element_type=jnp.float32)
        far_low = ring(behind[:, :half_cols], "heads", heads_n, 1)
        far_high = ring(ahead[:, half_cols:], "heads", heads_n, heads_n - 1)
        total = total + jnp.dot(behind, rows_of(1), preferred_element_type=jnp.float32)
        total = total + jnp.dot(ahead, rows_of(heads_n - 1), preferred_element_type=jnp.float32)
        far = jnp.concatenate([far_low, far_high], axis=1)
        total = total + jnp.dot(far, rows_of(2), preferred_element_type=jnp.float32)
        return total.astype(jnp.bfloat16)

    return local


def split_mesh(mesh):
    devices = mesh.devices
    heads_n, seq_n = devices.shape
    core_n = 2
    y_n = len({d.coords[1] for d in devices.flat})
    z_n = seq_n // (core_n * y_n)
    sizes = (heads_n, z_n, y_n, core_n)
    return Mesh(np.asarray(devices).reshape(sizes), ("heads",) + SEQ), sizes


def solution(mesh):
    sub, sizes = split_mesh(mesh)
    return jax.shard_map(
        make_local(sizes),
        mesh=sub,
        in_specs=(
            P(SEQ, "heads"),
            P(SEQ, "heads"),
            P(SEQ, "heads"),
            P(),
            P(),
            P("heads", None),
        ),
        out_specs=P(SEQ, "heads"),
        check_vma=False,
    )
```

```python
import math

import jax
import jax.numpy as jnp
import functools

import numpy as np
from jax import lax
from jax.experimental import pallas as pl
from jax.experimental.pallas import tpu as pltpu
from jax.sharding import Mesh
from jax.sharding import PartitionSpec as P

HEAD_SIZE = 128
BLOCK_TOKENS = 64
SEQ = ("z", "y", "core")


def shift(block, axis, size, distance):
    route = [(i, i + distance) for i in range(size) if 0 <= i + distance < size]
    return lax.ppermute(block, axis, route)


def ring(block, axis, size, distance):
    return lax.ppermute(block, axis, [(i, (i + distance) % size) for i in range(size)])


def spread(table, rows, cols):
    return jnp.repeat(jnp.repeat(table, rows, axis=-2), cols, axis=-1)


def vertical_kernel(slots_ref, q_ref, kv_hbm, key_tok_ref, query_tok_ref, top_ref, tot_ref, acc_ref,
                    o_ref, k_buf, v_buf, sems, *, scale):
    head = pl.program_id(0)
    heads = pl.num_programs(0)
    vert_count = k_buf.shape[1] // BLOCK_TOKENS

    def block_copies(h, buf_index):
        copies = []
        for n in range(vert_count):
            slot = slots_ref[h, n]
            rows = pl.ds(n * BLOCK_TOKENS, BLOCK_TOKENS)
            for part, buf in ((0, k_buf), (1, v_buf)):
                copies.append(
                    pltpu.make_async_copy(
                        kv_hbm.at[part, slot], buf.at[buf_index, rows], sems.at[buf_index, part, n]
                    )
                )
        return copies

    current = head % 2

    @pl.when(head == 0)
    def _():
        for copy in block_copies(0, 0):
            copy.start()

    @pl.when(head + 1 < heads)
    def _():
        for copy in block_copies(head + 1, 1 - current):
            copy.start()

    for copy in block_copies(head, current):
        copy.wait()
    s = lax.dot_general(
        q_ref[0], k_buf[current], (((1,), (1,)), ((), ())), preferred_element_type=jnp.float32
    ) * scale
    s = jnp.where(key_tok_ref[0] <= query_tok_ref[...], s, -jnp.inf)
    top_d = top_ref[0]
    top = jnp.maximum(top_d, jnp.max(s, axis=1, keepdims=True))
    p = jnp.exp(s - top)
    sc = jnp.exp(top_d - top)
    total = tot_ref[0] * sc + jnp.sum(p, axis=1, keepdims=True)
    acc = jnp.dot(p.astype(jnp.bfloat16), v_buf[current], preferred_element_type=jnp.float32)
    o_ref[...] = ((acc_ref[0] * sc + acc) / total).astype(o_ref.dtype)


def vertical_attention(slots, q, kv, key_tok, query_tok, top_d, tot_d, acc_d, interpret=False):
    heads, rows, dim = q.shape
    keys_n = key_tok.shape[-1]
    kernel = functools.partial(vertical_kernel, scale=1.0 / math.sqrt(dim))
    grid_spec = pltpu.PrefetchScalarGridSpec(
        num_scalar_prefetch=1,
        grid=(heads,),
        in_specs=[
            pl.BlockSpec((1, rows, dim), lambda i, t: (i, 0, 0)),
            pl.BlockSpec(memory_space=pl.ANY),
            pl.BlockSpec((1, 1, keys_n), lambda i, t: (i, 0, 0)),
            pl.BlockSpec((rows, 1), lambda i, t: (0, 0)),
            pl.BlockSpec((1, rows, 1), lambda i, t: (i, 0, 0)),
            pl.BlockSpec((1, rows, 1), lambda i, t: (i, 0, 0)),
            pl.BlockSpec((1, rows, dim), lambda i, t: (i, 0, 0)),
        ],
        out_specs=pl.BlockSpec((rows, dim), lambda i, t: (0, i)),
        scratch_shapes=[
            pltpu.VMEM((2, keys_n, dim), kv.dtype),
            pltpu.VMEM((2, keys_n, dim), kv.dtype),
            pltpu.SemaphoreType.DMA((2, 2, keys_n // BLOCK_TOKENS)),
        ],
    )
    return pl.pallas_call(
        kernel,
        grid_spec=grid_spec,
        out_shape=jax.ShapeDtypeStruct((rows, heads * dim), jnp.bfloat16),
        interpret=interpret,
    )(slots, q, kv, key_tok, query_tok, top_d, tot_d, acc_d)


def make_local(sizes):
    heads_n, z_n, y_n, core_n = sizes
    cycle_size = z_n * y_n * core_n

    def local(queries, keys, values, vertical, slash, out_weight):
        head_dim = HEAD_SIZE
        local_heads = queries.shape[1] // head_dim
        token_count = queries.shape[0]
        block_count = token_count // BLOCK_TOKENS
        score_scale = 1.0 / math.sqrt(head_dim)
        kv_group = lax.axis_index("heads")
        core = lax.axis_index("core")
        cycle_index = lax.axis_index(SEQ)

        vert_group = lax.dynamic_slice_in_dim(vertical, kv_group * local_heads, local_heads, 0)
        slash_group = lax.dynamic_slice_in_dim(slash, kv_group * local_heads, local_heads, 0)
        union_list = vert_group.reshape(-1)
        listed_count = union_list.shape[0]
        owner_dev = union_list // block_count
        within_dev = union_list % block_count
        paired = jnp.stack([keys, values]).reshape(2, block_count, BLOCK_TOKENS, head_dim)
        owned_here = owner_dev == cycle_index
        capacity = 2
        local_ids = jnp.arange(block_count, dtype=jnp.int32)
        owned_blocks = jnp.any(
            owned_here[None, :] & (within_dev[None, :] == local_ids[:, None]), axis=1
        )
        below = jnp.sum(
            (owned_blocks[None, :] & (local_ids[None, :] < local_ids[:, None])).astype(jnp.int32),
            axis=1,
        )
        owned_total = jnp.sum(owned_blocks.astype(jnp.int32))
        pick = jnp.stack(
            [owned_blocks & (below == 0), owned_blocks & (below == owned_total - 1)]
        ).astype(jnp.bfloat16)
        outgoing = jnp.einsum(
            "cb,kbtd->kctd", pick, paired, preferred_element_type=jnp.float32
        ).astype(jnp.bfloat16).reshape(2, capacity * BLOCK_TOKENS, head_dim)
        same_owner = (owner_dev[:, None] == owner_dev[None, :]) & (
            union_list[None, :] < union_list[:, None]
        )
        slot_index = jnp.sum(same_owner.astype(jnp.int32), axis=1)
        arrived = lax.all_gather(outgoing, SEQ, axis=1, tiled=True)

        rows_total, width = out_weight.shape
        col_width = width // heads_n
        half_rows = rows_total // core_n
        fetched = []
        for distance in range(1, heads_n):
            dest_cols = ((kv_group + distance) % heads_n) * col_width
            piece = lax.dynamic_slice(out_weight, (core * half_rows, dest_cols), (half_rows, col_width))
            fetched.append(ring(piece, "heads", heads_n, distance))
        fetched = jnp.stack(fetched)
        sibling_w = ring(fetched, "core", core_n, 1)
        own_w = lax.dynamic_slice(out_weight, (0, kv_group * col_width), (rows_total, col_width))

        earlier = shift(paired, SEQ, cycle_size, 1)
        farther = shift(paired, SEQ, cycle_size, 2)
        context = jnp.concatenate([farther, earlier, paired], axis=1)
        context_blocks = context.shape[1]
        context_k = context[0].reshape(context_blocks * BLOCK_TOKENS, head_dim)
        context_v = context[1].reshape(context_blocks * BLOCK_TOKENS, head_dim)
        first_block = cycle_index * block_count
        query_block = first_block + jnp.arange(block_count, dtype=jnp.int32)
        key_block = first_block - (context_blocks - block_count) + jnp.arange(
            context_blocks, dtype=jnp.int32
        )
        distance_blk = query_block[:, None] - key_block[None, :]
        token_pos = jnp.arange(BLOCK_TOKENS)
        causal_tri = token_pos[None, :] <= token_pos[:, None]
        causal_ctx = jnp.tile(causal_tri, (block_count, context_blocks))

        query_heads = queries.reshape(token_count, local_heads, head_dim).transpose(1, 0, 2)
        score_diag = (
            jnp.einsum("htd,ud->htu", query_heads, context_k, preferred_element_type=jnp.float32)
            * score_scale
        )
        in_slash = jnp.any(distance_blk[None, None] == slash_group[:, :, None, None], axis=1)
        in_vert = jnp.any(key_block[None, None, :] == vert_group[:, :, None], axis=1)
        keep_blk = in_slash & (key_block >= 0)[None, None, :] & jnp.logical_not(in_vert)[:, None, :]
        whole_blk = keep_blk & (distance_blk != 0)[None]
        allow_diag = spread(whole_blk, BLOCK_TOKENS, BLOCK_TOKENS) | (
            spread(keep_blk & (distance_blk == 0)[None], BLOCK_TOKENS, BLOCK_TOKENS)
            & causal_ctx[None]
        )
        top_diag = jnp.max(jnp.where(allow_diag, score_diag, -jnp.inf), axis=2, keepdims=True)
        expo_diag = jnp.where(allow_diag, jnp.exp(score_diag - top_diag), 0.0)
        total_diag = jnp.sum(expo_diag, axis=2, keepdims=True)
        acc_diag = jnp.einsum(
            "htu,ud->htd",
            expo_diag.astype(jnp.bfloat16),
            context_v,
            preferred_element_type=jnp.float32,
        )

        arrived = arrived.reshape(2, cycle_size * capacity, BLOCK_TOKENS, head_dim)
        vert_count = vert_group.shape[1]
        slots = (owner_dev * capacity + slot_index).reshape(local_heads, vert_count)
        key_tok = (vert_group[:, :, None] * BLOCK_TOKENS + token_pos).reshape(local_heads, 1, -1)
        query_tok = (first_block * BLOCK_TOKENS + jnp.arange(token_count, dtype=jnp.int32))[:, None]
        def rows_of(distance):
            mine, theirs = fetched[distance - 1], sibling_w[distance - 1]
            return jnp.where(
                core == 0,
                jnp.concatenate([mine, theirs], axis=0),
                jnp.concatenate([theirs, mine], axis=0),
            )

        pair_count = 2
        pair_heads = local_heads // pair_count
        pair_cols = pair_heads * head_dim
        weights = [own_w] + [rows_of(distance) for distance in range(1, heads_n)]
        total = None
        for pair in range(pair_count):
            heads_here = slice(pair * pair_heads, (pair + 1) * pair_heads)
            rows_here = slice(pair * pair_cols, (pair + 1) * pair_cols)
            attention = vertical_attention(
                slots[heads_here].astype(jnp.int32),
                query_heads[heads_here],
                arrived,
                key_tok[heads_here].astype(jnp.int32),
                query_tok,
                top_diag[heads_here],
                total_diag[heads_here],
                acc_diag[heads_here],
            )
            half_cols = pair_cols // 2
            behind = ring(attention, "heads", heads_n, 1)
            ahead = ring(attention, "heads", heads_n, heads_n - 1)
            far_low = ring(behind[:, :half_cols], "heads", heads_n, 1)
            far_high = ring(ahead[:, half_cols:], "heads", heads_n, heads_n - 1)
            part = jnp.dot(attention, weights[0][rows_here], preferred_element_type=jnp.float32)
            total = part if total is None else total + part
            total = total + jnp.dot(behind, weights[1][rows_here], preferred_element_type=jnp.float32)
            total = total + jnp.dot(
                ahead, weights[heads_n - 1][rows_here], preferred_element_type=jnp.float32
            )
            far = jnp.concatenate([far_low, far_high], axis=1)
            total = total + jnp.dot(far, weights[2][rows_here], preferred_element_type=jnp.float32)
        return total.astype(jnp.bfloat16)

    return local


def split_mesh(mesh):
    devices = mesh.devices
    heads_n, seq_n = devices.shape
    core_n = 2
    y_n = len({d.coords[1] for d in devices.flat})
    z_n = seq_n // (core_n * y_n)
    sizes = (heads_n, z_n, y_n, core_n)
    return Mesh(np.asarray(devices).reshape(sizes), ("heads",) + SEQ), sizes


def solution(mesh):
    sub, sizes = split_mesh(mesh)
    return jax.shard_map(
        make_local(sizes),
        mesh=sub,
        in_specs=(
            P(SEQ, "heads"),
            P(SEQ, "heads"),
            P(SEQ, "heads"),
            P(),
            P(),
            P("heads", None),
        ),
        out_specs=P(SEQ, "heads"),
        check_vma=False,
    )
```

```python
import math

import jax
import jax.numpy as jnp
import functools

import numpy as np
from jax import lax
from jax.experimental import pallas as pl
from jax.experimental.pallas import tpu as pltpu
from jax.sharding import Mesh
from jax.sharding import PartitionSpec as P

HEAD_SIZE = 128
BLOCK_TOKENS = 64
SEQ = ("z", "y", "core")


def shift(block, axis, size, distance):
    route = [(i, i + distance) for i in range(size) if 0 <= i + distance < size]
    return lax.ppermute(block, axis, route)


def ring(block, axis, size, distance):
    return lax.ppermute(block, axis, [(i, (i + distance) % size) for i in range(size)])


def spread(table, rows, cols):
    return jnp.repeat(jnp.repeat(table, rows, axis=-2), cols, axis=-1)


def vertical_kernel(slots_ref, q_ref, kv_hbm, key_tok_ref, query_tok_ref, top_ref, tot_ref, acc_ref,
                    o_ref, k_buf, v_buf, sems, *, scale):
    head = pl.program_id(0)
    heads = pl.num_programs(0)
    vert_count = k_buf.shape[1] // BLOCK_TOKENS

    def block_copies(h, buf_index):
        copies = []
        for n in range(vert_count):
            slot = slots_ref[h, n]
            rows = pl.ds(n * BLOCK_TOKENS, BLOCK_TOKENS)
            for part, buf in ((0, k_buf), (1, v_buf)):
                copies.append(
                    pltpu.make_async_copy(
                        kv_hbm.at[part, slot], buf.at[buf_index, rows], sems.at[buf_index, part, n]
                    )
                )
        return copies

    current = head % 2

    @pl.when(head == 0)
    def _():
        for copy in block_copies(0, 0):
            copy.start()

    for copy in block_copies(head, current):
        copy.wait()

    @pl.when(head + 1 < heads)
    def _():
        for copy in block_copies(head + 1, 1 - current):
            copy.start()

    s = lax.dot_general(
        q_ref[0], k_buf[current], (((1,), (1,)), ((), ())), preferred_element_type=jnp.float32
    ) * scale
    s = jnp.where(key_tok_ref[0] <= query_tok_ref[...], s, -jnp.inf)
    top_d = top_ref[0]
    top = jnp.maximum(top_d, jnp.max(s, axis=1, keepdims=True))
    p = jnp.exp(s - top)
    sc = jnp.exp(top_d - top)
    total = tot_ref[0] * sc + jnp.sum(p, axis=1, keepdims=True)
    acc = jnp.dot(p.astype(jnp.bfloat16), v_buf[current], preferred_element_type=jnp.float32)
    o_ref[...] = ((acc_ref[0] * sc + acc) / total).astype(o_ref.dtype)


def vertical_attention(slots, q, kv, key_tok, query_tok, top_d, tot_d, acc_d, interpret=False):
    heads, rows, dim = q.shape
    keys_n = key_tok.shape[-1]
    kernel = functools.partial(vertical_kernel, scale=1.0 / math.sqrt(dim))
    grid_spec = pltpu.PrefetchScalarGridSpec(
        num_scalar_prefetch=1,
        grid=(heads,),
        in_specs=[
            pl.BlockSpec((1, rows, dim), lambda i, t: (i, 0, 0)),
            pl.BlockSpec(memory_space=pl.ANY),
            pl.BlockSpec((1, 1, keys_n), lambda i, t: (i, 0, 0)),
            pl.BlockSpec((rows, 1), lambda i, t: (0, 0)),
            pl.BlockSpec((1, rows, 1), lambda i, t: (i, 0, 0)),
            pl.BlockSpec((1, rows, 1), lambda i, t: (i, 0, 0)),
            pl.BlockSpec((1, rows, dim), lambda i, t: (i, 0, 0)),
        ],
        out_specs=pl.BlockSpec((rows, dim), lambda i, t: (0, i)),
        scratch_shapes=[
            pltpu.VMEM((2, keys_n, dim), kv.dtype),
            pltpu.VMEM((2, keys_n, dim), kv.dtype),
            pltpu.SemaphoreType.DMA((2, 2, keys_n // BLOCK_TOKENS)),
        ],
    )
    return pl.pallas_call(
        kernel,
        grid_spec=grid_spec,
        out_shape=jax.ShapeDtypeStruct((rows, heads * dim), jnp.bfloat16),
        interpret=interpret,
    )(slots, q, kv, key_tok, query_tok, top_d, tot_d, acc_d)


def make_local(sizes):
    heads_n, z_n, y_n, core_n = sizes
    cycle_size = z_n * y_n * core_n

    def local(queries, keys, values, vertical, slash, out_weight):
        head_dim = HEAD_SIZE
        local_heads = queries.shape[1] // head_dim
        token_count = queries.shape[0]
        block_count = token_count // BLOCK_TOKENS
        score_scale = 1.0 / math.sqrt(head_dim)
        kv_group = lax.axis_index("heads")
        core = lax.axis_index("core")
        cycle_index = lax.axis_index(SEQ)

        vert_group = lax.dynamic_slice_in_dim(vertical, kv_group * local_heads, local_heads, 0)
        slash_group = lax.dynamic_slice_in_dim(slash, kv_group * local_heads, local_heads, 0)
        union_list = vert_group.reshape(-1)
        listed_count = union_list.shape[0]
        owner_dev = union_list // block_count
        within_dev = union_list % block_count
        paired = jnp.stack([keys, values]).reshape(2, block_count, BLOCK_TOKENS, head_dim)
        owned_here = owner_dev == cycle_index
        capacity = 2
        local_ids = jnp.arange(block_count, dtype=jnp.int32)
        owned_blocks = jnp.any(
            owned_here[None, :] & (within_dev[None, :] == local_ids[:, None]), axis=1
        )
        below = jnp.sum(
            (owned_blocks[None, :] & (local_ids[None, :] < local_ids[:, None])).astype(jnp.int32),
            axis=1,
        )
        owned_total = jnp.sum(owned_blocks.astype(jnp.int32))
        pick = jnp.stack(
            [owned_blocks & (below == 0), owned_blocks & (below == owned_total - 1)]
        ).astype(jnp.bfloat16)
        outgoing = jnp.stack(
            [
                jnp.einsum(
                    "cb,btd->ctd",
                    pick,
                    part.reshape(block_count, BLOCK_TOKENS, head_dim),
                    preferred_element_type=jnp.float32,
                ).astype(jnp.bfloat16)
                for part in (keys, values)
            ]
        ).reshape(2, capacity * BLOCK_TOKENS, head_dim)
        same_owner = (owner_dev[:, None] == owner_dev[None, :]) & (
            union_list[None, :] < union_list[:, None]
        )
        slot_index = jnp.sum(same_owner.astype(jnp.int32), axis=1)
        arrived = lax.all_gather(outgoing, SEQ, axis=1, tiled=True)

        rows_total, width = out_weight.shape
        col_width = width // heads_n
        half_rows = rows_total // core_n
        fetched = []
        for distance in range(1, heads_n):
            dest_cols = ((kv_group + distance) % heads_n) * col_width
            piece = lax.dynamic_slice(out_weight, (core * half_rows, dest_cols), (half_rows, col_width))
            fetched.append(ring(piece, "heads", heads_n, distance))
        fetched = jnp.stack(fetched)
        sibling_w = ring(fetched, "core", core_n, 1)
        own_w = lax.dynamic_slice(out_weight, (0, kv_group * col_width), (rows_total, col_width))

        earlier = shift(paired, SEQ, cycle_size, 1)
        farther = shift(paired, SEQ, cycle_size, 2)
        context = jnp.concatenate([farther, earlier, paired], axis=1)
        context_blocks = context.shape[1]
        context_k = context[0].reshape(context_blocks * BLOCK_TOKENS, head_dim)
        context_v = context[1].reshape(context_blocks * BLOCK_TOKENS, head_dim)
        first_block = cycle_index * block_count
        query_block = first_block + jnp.arange(block_count, dtype=jnp.int32)
        key_block = first_block - (context_blocks - block_count) + jnp.arange(
            context_blocks, dtype=jnp.int32
        )
        distance_blk = query_block[:, None] - key_block[None, :]
        token_pos = jnp.arange(BLOCK_TOKENS)
        causal_tri = token_pos[None, :] <= token_pos[:, None]
        causal_ctx = jnp.tile(causal_tri, (block_count, context_blocks))

        query_heads = queries.reshape(token_count, local_heads, head_dim).transpose(1, 0, 2)
        score_diag = (
            jnp.einsum("htd,ud->htu", query_heads, context_k, preferred_element_type=jnp.float32)
            * score_scale
        )
        in_slash = jnp.any(distance_blk[None, None] == slash_group[:, :, None, None], axis=1)
        in_vert = jnp.any(key_block[None, None, :] == vert_group[:, :, None], axis=1)
        keep_blk = in_slash & (key_block >= 0)[None, None, :] & jnp.logical_not(in_vert)[:, None, :]
        whole_blk = keep_blk & (distance_blk != 0)[None]
        allow_diag = spread(whole_blk, BLOCK_TOKENS, BLOCK_TOKENS) | (
            spread(keep_blk & (distance_blk == 0)[None], BLOCK_TOKENS, BLOCK_TOKENS)
            & causal_ctx[None]
        )
        top_diag = jnp.max(jnp.where(allow_diag, score_diag, -jnp.inf), axis=2, keepdims=True)
        expo_diag = jnp.where(allow_diag, jnp.exp(score_diag - top_diag), 0.0)
        total_diag = jnp.sum(expo_diag, axis=2, keepdims=True)
        acc_diag = jnp.einsum(
            "htu,ud->htd",
            expo_diag.astype(jnp.bfloat16),
            context_v,
            preferred_element_type=jnp.float32,
        )

        arrived = arrived.reshape(2, cycle_size * capacity, BLOCK_TOKENS, head_dim)
        vert_count = vert_group.shape[1]
        slots = (owner_dev * capacity + slot_index).reshape(local_heads, vert_count)
        key_tok = (vert_group[:, :, None] * BLOCK_TOKENS + token_pos).reshape(local_heads, 1, -1)
        query_tok = (first_block * BLOCK_TOKENS + jnp.arange(token_count, dtype=jnp.int32))[:, None]
        attention = vertical_attention(
            slots.astype(jnp.int32),
            query_heads,
            arrived,
            key_tok.astype(jnp.int32),
            query_tok,
            top_diag,
            total_diag,
            acc_diag,
        )

        def rows_of(distance):
            mine, theirs = fetched[distance - 1], sibling_w[distance - 1]
            return jnp.where(
                core == 0,
                jnp.concatenate([mine, theirs], axis=0),
                jnp.concatenate([theirs, mine], axis=0),
            )

        half_cols = attention.shape[1] // 2
        behind = ring(attention, "heads", heads_n, 1)
        ahead = ring(attention, "heads", heads_n, heads_n - 1)
        total = jnp.dot(attention, own_w, preferred_element_type=jnp.float32)
        far_low = ring(behind[:, :half_cols], "heads", heads_n, 1)
        far_high = ring(ahead[:, half_cols:], "heads", heads_n, heads_n - 1)
        total = total + jnp.dot(behind, rows_of(1), preferred_element_type=jnp.float32)
        total = total + jnp.dot(ahead, rows_of(heads_n - 1), preferred_element_type=jnp.float32)
        far = jnp.concatenate([far_low, far_high], axis=1)
        total = total + jnp.dot(far, rows_of(2), preferred_element_type=jnp.float32)
        return total.astype(jnp.bfloat16)

    return local


def split_mesh(mesh):
    devices = mesh.devices
    heads_n, seq_n = devices.shape
    core_n = 2
    y_n = len({d.coords[1] for d in devices.flat})
    z_n = seq_n // (core_n * y_n)
    sizes = (heads_n, z_n, y_n, core_n)
    return Mesh(np.asarray(devices).reshape(sizes), ("heads",) + SEQ), sizes


def solution(mesh):
    sub, sizes = split_mesh(mesh)
    return jax.shard_map(
        make_local(sizes),
        mesh=sub,
        in_specs=(
            P(SEQ, "heads"),
            P(SEQ, "heads"),
            P(SEQ, "heads"),
            P(),
            P(),
            P("heads", None),
        ),
        out_specs=P(SEQ, "heads"),
        check_vma=False,
    )
```

```python
import math

import jax
import jax.numpy as jnp
import functools

import numpy as np
from jax import lax
from jax.experimental import pallas as pl
from jax.experimental.pallas import tpu as pltpu
from jax.sharding import Mesh
from jax.sharding import PartitionSpec as P

HEAD_SIZE = 128
BLOCK_TOKENS = 64
SEQ = ("z", "y", "core")


def shift(block, axis, size, distance):
    route = [(i, i + distance) for i in range(size) if 0 <= i + distance < size]
    return lax.ppermute(block, axis, route)


def ring(block, axis, size, distance):
    return lax.ppermute(block, axis, [(i, (i + distance) % size) for i in range(size)])


def spread(table, rows, cols):
    return jnp.repeat(jnp.repeat(table, rows, axis=-2), cols, axis=-1)


def vertical_kernel(slots_ref, q_ref, kv_hbm, key_tok_ref, query_tok_ref, top_ref, tot_ref, acc_ref,
                    o_ref, k_buf, v_buf, sems, *, scale):
    head = pl.program_id(0)
    heads = pl.num_programs(0)
    vert_count = k_buf.shape[1] // BLOCK_TOKENS

    def block_copies(h, buf_index):
        copies = []
        for n in range(vert_count):
            slot = slots_ref[h, n]
            rows = pl.ds(n * BLOCK_TOKENS, BLOCK_TOKENS)
            for part, buf in ((0, k_buf), (1, v_buf)):
                copies.append(
                    pltpu.make_async_copy(
                        kv_hbm.at[part, slot], buf.at[buf_index, rows], sems.at[buf_index, part, n]
                    )
                )
        return copies

    current = head % 2

    @pl.when(head == 0)
    def _():
        for copy in block_copies(0, 0):
            copy.start()

    for copy in block_copies(head, current):
        copy.wait()

    @pl.when(head + 1 < heads)
    def _():
        for copy in block_copies(head + 1, 1 - current):
            copy.start()

    s = lax.dot_general(
        q_ref[0], k_buf[current], (((1,), (1,)), ((), ())), preferred_element_type=jnp.float32
    ) * scale
    s = jnp.where(key_tok_ref[0] <= query_tok_ref[...], s, -jnp.inf)
    top_d = top_ref[0]
    top = jnp.maximum(top_d, jnp.max(s, axis=1, keepdims=True))
    p = jnp.exp(s - top)
    sc = jnp.exp(top_d - top)
    total = tot_ref[0] * sc + jnp.sum(p, axis=1, keepdims=True)
    acc = jnp.dot(p.astype(jnp.bfloat16), v_buf[current], preferred_element_type=jnp.float32)
    o_ref[...] = ((acc_ref[0] * sc + acc) / total).astype(o_ref.dtype)


def vertical_attention(slots, q, kv, key_tok, query_tok, top_d, tot_d, acc_d, interpret=False):
    heads, rows, dim = q.shape
    keys_n = key_tok.shape[-1]
    kernel = functools.partial(vertical_kernel, scale=1.0 / math.sqrt(dim))
    grid_spec = pltpu.PrefetchScalarGridSpec(
        num_scalar_prefetch=1,
        grid=(heads,),
        in_specs=[
            pl.BlockSpec((1, rows, dim), lambda i, t: (i, 0, 0)),
            pl.BlockSpec(memory_space=pl.ANY),
            pl.BlockSpec((1, 1, keys_n), lambda i, t: (i, 0, 0)),
            pl.BlockSpec((rows, 1), lambda i, t: (0, 0)),
            pl.BlockSpec((1, rows, 1), lambda i, t: (i, 0, 0)),
            pl.BlockSpec((1, rows, 1), lambda i, t: (i, 0, 0)),
            pl.BlockSpec((1, rows, dim), lambda i, t: (i, 0, 0)),
        ],
        out_specs=pl.BlockSpec((rows, dim), lambda i, t: (0, i)),
        scratch_shapes=[
            pltpu.VMEM((2, keys_n, dim), kv.dtype),
            pltpu.VMEM((2, keys_n, dim), kv.dtype),
            pltpu.SemaphoreType.DMA((2, 2, keys_n // BLOCK_TOKENS)),
        ],
    )
    return pl.pallas_call(
        kernel,
        grid_spec=grid_spec,
        out_shape=jax.ShapeDtypeStruct((rows, heads * dim), jnp.bfloat16),
        interpret=interpret,
    )(slots, q, kv, key_tok, query_tok, top_d, tot_d, acc_d)


def make_local(sizes):
    heads_n, z_n, y_n, core_n = sizes
    cycle_size = z_n * y_n * core_n

    def local(queries, keys, values, vertical, slash, out_weight):
        head_dim = HEAD_SIZE
        local_heads = queries.shape[1] // head_dim
        token_count = queries.shape[0]
        block_count = token_count // BLOCK_TOKENS
        score_scale = 1.0 / math.sqrt(head_dim)
        kv_group = lax.axis_index("heads")
        core = lax.axis_index("core")
        cycle_index = lax.axis_index(SEQ)

        vert_group = lax.dynamic_slice_in_dim(vertical, kv_group * local_heads, local_heads, 0)
        slash_group = lax.dynamic_slice_in_dim(slash, kv_group * local_heads, local_heads, 0)
        union_list = vert_group.reshape(-1)
        listed_count = union_list.shape[0]
        owner_dev = union_list // block_count
        within_dev = union_list % block_count
        paired = jnp.stack([keys, values]).reshape(2, block_count, BLOCK_TOKENS, head_dim)
        owned_here = owner_dev == cycle_index
        capacity = 2
        local_ids = jnp.arange(block_count, dtype=jnp.int32)
        owned_blocks = jnp.any(
            owned_here[None, :] & (within_dev[None, :] == local_ids[:, None]), axis=1
        )
        below = jnp.sum(
            (owned_blocks[None, :] & (local_ids[None, :] < local_ids[:, None])).astype(jnp.int32),
            axis=1,
        )
        owned_total = jnp.sum(owned_blocks.astype(jnp.int32))
        pick = jnp.stack([owned_blocks & (below == 0), owned_blocks & (below == owned_total - 1)])

        def picked(part):
            blocks = part.reshape(block_count, BLOCK_TOKENS, head_dim).astype(jnp.float32)
            chosen_blocks = jnp.where(pick[:, :, None, None], blocks[None], 0.0)
            return jnp.sum(chosen_blocks, axis=1).astype(part.dtype)

        outgoing = jnp.stack([picked(keys), picked(values)]).reshape(
            2, capacity * BLOCK_TOKENS, head_dim
        )
        same_owner = (owner_dev[:, None] == owner_dev[None, :]) & (
            union_list[None, :] < union_list[:, None]
        )
        slot_index = jnp.sum(same_owner.astype(jnp.int32), axis=1)
        arrived = lax.all_gather(outgoing, SEQ, axis=1, tiled=True)

        rows_total, width = out_weight.shape
        col_width = width // heads_n
        half_rows = rows_total // core_n
        fetched = []
        for distance in range(1, heads_n):
            dest_cols = ((kv_group + distance) % heads_n) * col_width
            piece = lax.dynamic_slice(out_weight, (core * half_rows, dest_cols), (half_rows, col_width))
            fetched.append(ring(piece, "heads", heads_n, distance))
        fetched = jnp.stack(fetched)
        sibling_w = ring(fetched, "core", core_n, 1)
        own_w = lax.dynamic_slice(out_weight, (0, kv_group * col_width), (rows_total, col_width))

        earlier = shift(paired, SEQ, cycle_size, 1)
        farther = shift(paired, SEQ, cycle_size, 2)
        context = jnp.concatenate([farther, earlier, paired], axis=1)
        context_blocks = context.shape[1]
        context_k = context[0].reshape(context_blocks * BLOCK_TOKENS, head_dim)
        context_v = context[1].reshape(context_blocks * BLOCK_TOKENS, head_dim)
        first_block = cycle_index * block_count
        query_block = first_block + jnp.arange(block_count, dtype=jnp.int32)
        key_block = first_block - (context_blocks - block_count) + jnp.arange(
            context_blocks, dtype=jnp.int32
        )
        distance_blk = query_block[:, None] - key_block[None, :]
        token_pos = jnp.arange(BLOCK_TOKENS)
        causal_tri = token_pos[None, :] <= token_pos[:, None]
        causal_ctx = jnp.tile(causal_tri, (block_count, context_blocks))

        query_heads = queries.reshape(token_count, local_heads, head_dim).transpose(1, 0, 2)
        score_diag = (
            jnp.einsum("htd,ud->htu", query_heads, context_k, preferred_element_type=jnp.float32)
            * score_scale
        )
        in_slash = jnp.any(distance_blk[None, None] == slash_group[:, :, None, None], axis=1)
        in_vert = jnp.any(key_block[None, None, :] == vert_group[:, :, None], axis=1)
        keep_blk = in_slash & (key_block >= 0)[None, None, :] & jnp.logical_not(in_vert)[:, None, :]
        whole_blk = keep_blk & (distance_blk != 0)[None]
        allow_diag = spread(whole_blk, BLOCK_TOKENS, BLOCK_TOKENS) | (
            spread(keep_blk & (distance_blk == 0)[None], BLOCK_TOKENS, BLOCK_TOKENS)
            & causal_ctx[None]
        )
        top_diag = jnp.max(jnp.where(allow_diag, score_diag, -jnp.inf), axis=2, keepdims=True)
        expo_diag = jnp.where(allow_diag, jnp.exp(score_diag - top_diag), 0.0)
        total_diag = jnp.sum(expo_diag, axis=2, keepdims=True)
        acc_diag = jnp.einsum(
            "htu,ud->htd",
            expo_diag.astype(jnp.bfloat16),
            context_v,
            preferred_element_type=jnp.float32,
        )

        arrived = arrived.reshape(2, cycle_size * capacity, BLOCK_TOKENS, head_dim)
        vert_count = vert_group.shape[1]
        slots = (owner_dev * capacity + slot_index).reshape(local_heads, vert_count)
        key_tok = (vert_group[:, :, None] * BLOCK_TOKENS + token_pos).reshape(local_heads, 1, -1)
        query_tok = (first_block * BLOCK_TOKENS + jnp.arange(token_count, dtype=jnp.int32))[:, None]
        attention = vertical_attention(
            slots.astype(jnp.int32),
            query_heads,
            arrived,
            key_tok.astype(jnp.int32),
            query_tok,
            top_diag,
            total_diag,
            acc_diag,
        )

        def rows_of(distance):
            mine, theirs = fetched[distance - 1], sibling_w[distance - 1]
            return jnp.where(
                core == 0,
                jnp.concatenate([mine, theirs], axis=0),
                jnp.concatenate([theirs, mine], axis=0),
            )

        half_cols = attention.shape[1] // 2
        behind = ring(attention, "heads", heads_n, 1)
        ahead = ring(attention, "heads", heads_n, heads_n - 1)
        total = jnp.dot(attention, own_w, preferred_element_type=jnp.float32)
        far_low = ring(behind[:, :half_cols], "heads", heads_n, 1)
        far_high = ring(ahead[:, half_cols:], "heads", heads_n, heads_n - 1)
        total = total + jnp.dot(behind, rows_of(1), preferred_element_type=jnp.float32)
        total = total + jnp.dot(ahead, rows_of(heads_n - 1), preferred_element_type=jnp.float32)
        far = jnp.concatenate([far_low, far_high], axis=1)
        total = total + jnp.dot(far, rows_of(2), preferred_element_type=jnp.float32)
        return total.astype(jnp.bfloat16)

    return local


def split_mesh(mesh):
    devices = mesh.devices
    heads_n, seq_n = devices.shape
    core_n = 2
    y_n = len({d.coords[1] for d in devices.flat})
    z_n = seq_n // (core_n * y_n)
    sizes = (heads_n, z_n, y_n, core_n)
    return Mesh(np.asarray(devices).reshape(sizes), ("heads",) + SEQ), sizes


def solution(mesh):
    sub, sizes = split_mesh(mesh)
    return jax.shard_map(
        make_local(sizes),
        mesh=sub,
        in_specs=(
            P(SEQ, "heads"),
            P(SEQ, "heads"),
            P(SEQ, "heads"),
            P(),
            P(),
            P("heads", None),
        ),
        out_specs=P(SEQ, "heads"),
        check_vma=False,
    )
```

```python
import math

import jax
import jax.numpy as jnp
import functools

import numpy as np
from jax import lax
from jax.experimental import pallas as pl
from jax.experimental.pallas import tpu as pltpu
from jax.sharding import Mesh
from jax.sharding import PartitionSpec as P

HEAD_SIZE = 128
BLOCK_TOKENS = 64
SEQ = ("z", "y", "core")


def shift(block, axis, size, distance):
    route = [(i, i + distance) for i in range(size) if 0 <= i + distance < size]
    return lax.ppermute(block, axis, route)


def ring(block, axis, size, distance):
    return lax.ppermute(block, axis, [(i, (i + distance) % size) for i in range(size)])


def spread(table, rows, cols):
    return jnp.repeat(jnp.repeat(table, rows, axis=-2), cols, axis=-1)


def vertical_kernel(slots_ref, q_ref, kv_hbm, key_tok_ref, query_tok_ref, acc_ref,
                    o_ref, k_buf, v_buf, sems, *, scale):
    head = pl.program_id(0)
    heads = pl.num_programs(0)
    vert_count = k_buf.shape[1] // BLOCK_TOKENS

    def block_copies(h, buf_index):
        copies = []
        for n in range(vert_count):
            slot = slots_ref[h, n]
            rows = pl.ds(n * BLOCK_TOKENS, BLOCK_TOKENS)
            for part, buf in ((0, k_buf), (1, v_buf)):
                copies.append(
                    pltpu.make_async_copy(
                        kv_hbm.at[part, slot], buf.at[buf_index, rows], sems.at[buf_index, part, n]
                    )
                )
        return copies

    current = head % 2

    @pl.when(head == 0)
    def _():
        for copy in block_copies(0, 0):
            copy.start()

    for copy in block_copies(head, current):
        copy.wait()

    @pl.when(head + 1 < heads)
    def _():
        for copy in block_copies(head + 1, 1 - current):
            copy.start()

    s = lax.dot_general(
        q_ref[0], k_buf[current], (((1,), (1,)), ((), ())), preferred_element_type=jnp.float32
    ) * scale
    s = jnp.where(key_tok_ref[0] <= query_tok_ref[...], s, -jnp.inf)
    dim = q_ref.shape[-1]
    top_d = acc_ref[0, :, dim:dim + 1]
    top = jnp.maximum(top_d, jnp.max(s, axis=1, keepdims=True))
    p = jnp.exp(s - top)
    sc = jnp.exp(top_d - top)
    total = acc_ref[0, :, dim + 1:dim + 2] * sc + jnp.sum(p, axis=1, keepdims=True)
    acc = jnp.dot(p.astype(jnp.bfloat16), v_buf[current], preferred_element_type=jnp.float32)
    o_ref[...] = ((acc_ref[0, :, :dim] * sc + acc) / total).astype(o_ref.dtype)


def vertical_attention(slots, q, kv, key_tok, query_tok, top_d, tot_d, acc_d, interpret=False):
    spare = jnp.zeros(acc_d.shape[:-1] + (acc_d.shape[-1] - 2,), acc_d.dtype)
    acc_d = jnp.concatenate([acc_d, top_d, tot_d, spare], axis=-1)
    heads, rows, dim = q.shape
    keys_n = key_tok.shape[-1]
    kernel = functools.partial(vertical_kernel, scale=1.0 / math.sqrt(dim))
    grid_spec = pltpu.PrefetchScalarGridSpec(
        num_scalar_prefetch=1,
        grid=(heads,),
        in_specs=[
            pl.BlockSpec((1, rows, dim), lambda i, t: (i, 0, 0)),
            pl.BlockSpec(memory_space=pl.ANY),
            pl.BlockSpec((1, 1, keys_n), lambda i, t: (i, 0, 0)),
            pl.BlockSpec((rows, 1), lambda i, t: (0, 0)),
            pl.BlockSpec((1, rows, 2 * dim), lambda i, t: (i, 0, 0)),
        ],
        out_specs=pl.BlockSpec((rows, dim), lambda i, t: (0, i)),
        scratch_shapes=[
            pltpu.VMEM((2, keys_n, dim), kv.dtype),
            pltpu.VMEM((2, keys_n, dim), kv.dtype),
            pltpu.SemaphoreType.DMA((2, 2, keys_n // BLOCK_TOKENS)),
        ],
    )
    return pl.pallas_call(
        kernel,
        grid_spec=grid_spec,
        out_shape=jax.ShapeDtypeStruct((rows, heads * dim), jnp.bfloat16),
        interpret=interpret,
    )(slots, q, kv, key_tok, query_tok, acc_d)


def make_local(sizes):
    heads_n, z_n, y_n, core_n = sizes
    cycle_size = z_n * y_n * core_n

    def local(queries, keys, values, vertical, slash, out_weight):
        head_dim = HEAD_SIZE
        local_heads = queries.shape[1] // head_dim
        token_count = queries.shape[0]
        block_count = token_count // BLOCK_TOKENS
        score_scale = 1.0 / math.sqrt(head_dim)
        kv_group = lax.axis_index("heads")
        core = lax.axis_index("core")
        cycle_index = lax.axis_index(SEQ)

        vert_group = lax.dynamic_slice_in_dim(vertical, kv_group * local_heads, local_heads, 0)
        slash_group = lax.dynamic_slice_in_dim(slash, kv_group * local_heads, local_heads, 0)
        union_list = vert_group.reshape(-1)
        listed_count = union_list.shape[0]
        owner_dev = union_list // block_count
        within_dev = union_list % block_count
        paired = jnp.stack([keys, values]).reshape(2, block_count, BLOCK_TOKENS, head_dim)
        owned_here = owner_dev == cycle_index
        capacity = 2
        local_ids = jnp.arange(block_count, dtype=jnp.int32)
        owned_blocks = jnp.any(
            owned_here[None, :] & (within_dev[None, :] == local_ids[:, None]), axis=1
        )
        below = jnp.sum(
            (owned_blocks[None, :] & (local_ids[None, :] < local_ids[:, None])).astype(jnp.int32),
            axis=1,
        )
        owned_total = jnp.sum(owned_blocks.astype(jnp.int32))
        pick = jnp.stack([owned_blocks & (below == 0), owned_blocks & (below == owned_total - 1)])

        def picked(part):
            blocks = part.reshape(block_count, BLOCK_TOKENS, head_dim).astype(jnp.float32)
            chosen_blocks = jnp.where(pick[:, :, None, None], blocks[None], 0.0)
            return jnp.sum(chosen_blocks, axis=1).astype(part.dtype)

        outgoing = jnp.stack([picked(keys), picked(values)]).reshape(
            2, capacity * BLOCK_TOKENS, head_dim
        )
        same_owner = (owner_dev[:, None] == owner_dev[None, :]) & (
            union_list[None, :] < union_list[:, None]
        )
        slot_index = jnp.sum(same_owner.astype(jnp.int32), axis=1)
        arrived = lax.all_gather(outgoing, SEQ, axis=1, tiled=True)

        rows_total, width = out_weight.shape
        col_width = width // heads_n
        half_rows = rows_total // core_n
        fetched = []
        for distance in range(1, heads_n):
            dest_cols = ((kv_group + distance) % heads_n) * col_width
            piece = lax.dynamic_slice(out_weight, (core * half_rows, dest_cols), (half_rows, col_width))
            fetched.append(ring(piece, "heads", heads_n, distance))
        fetched = jnp.stack(fetched)
        sibling_w = ring(fetched, "core", core_n, 1)
        own_w = lax.dynamic_slice(out_weight, (0, kv_group * col_width), (rows_total, col_width))

        earlier = shift(paired, SEQ, cycle_size, 1)
        farther = shift(paired, SEQ, cycle_size, 2)
        context = jnp.concatenate([farther, earlier, paired], axis=1)
        context_blocks = context.shape[1]
        context_k = context[0].reshape(context_blocks * BLOCK_TOKENS, head_dim)
        context_v = context[1].reshape(context_blocks * BLOCK_TOKENS, head_dim)
        first_block = cycle_index * block_count
        query_block = first_block + jnp.arange(block_count, dtype=jnp.int32)
        key_block = first_block - (context_blocks - block_count) + jnp.arange(
            context_blocks, dtype=jnp.int32
        )
        distance_blk = query_block[:, None] - key_block[None, :]
        token_pos = jnp.arange(BLOCK_TOKENS)
        causal_tri = token_pos[None, :] <= token_pos[:, None]
        causal_ctx = jnp.tile(causal_tri, (block_count, context_blocks))

        query_heads = queries.reshape(token_count, local_heads, head_dim).transpose(1, 0, 2)
        score_diag = (
            jnp.einsum("htd,ud->htu", query_heads, context_k, preferred_element_type=jnp.float32)
            * score_scale
        )
        in_slash = jnp.any(distance_blk[None, None] == slash_group[:, :, None, None], axis=1)
        in_vert = jnp.any(key_block[None, None, :] == vert_group[:, :, None], axis=1)
        keep_blk = in_slash & (key_block >= 0)[None, None, :] & jnp.logical_not(in_vert)[:, None, :]
        whole_blk = keep_blk & (distance_blk != 0)[None]
        allow_diag = spread(whole_blk, BLOCK_TOKENS, BLOCK_TOKENS) | (
            spread(keep_blk & (distance_blk == 0)[None], BLOCK_TOKENS, BLOCK_TOKENS)
            & causal_ctx[None]
        )
        top_diag = jnp.max(jnp.where(allow_diag, score_diag, -jnp.inf), axis=2, keepdims=True)
        expo_diag = jnp.where(allow_diag, jnp.exp(score_diag - top_diag), 0.0)
        total_diag = jnp.sum(expo_diag, axis=2, keepdims=True)
        acc_diag = jnp.einsum(
            "htu,ud->htd",
            expo_diag.astype(jnp.bfloat16),
            context_v,
            preferred_element_type=jnp.float32,
        )

        arrived = arrived.reshape(2, cycle_size * capacity, BLOCK_TOKENS, head_dim)
        vert_count = vert_group.shape[1]
        slots = (owner_dev * capacity + slot_index).reshape(local_heads, vert_count)
        key_tok = (vert_group[:, :, None] * BLOCK_TOKENS + token_pos).reshape(local_heads, 1, -1)
        query_tok = (first_block * BLOCK_TOKENS + jnp.arange(token_count, dtype=jnp.int32))[:, None]
        attention = vertical_attention(
            slots.astype(jnp.int32),
            query_heads,
            arrived,
            key_tok.astype(jnp.int32),
            query_tok,
            top_diag,
            total_diag,
            acc_diag,
        )

        def rows_of(distance):
            mine, theirs = fetched[distance - 1], sibling_w[distance - 1]
            return jnp.where(
                core == 0,
                jnp.concatenate([mine, theirs], axis=0),
                jnp.concatenate([theirs, mine], axis=0),
            )

        half_cols = attention.shape[1] // 2
        behind = ring(attention, "heads", heads_n, 1)
        ahead = ring(attention, "heads", heads_n, heads_n - 1)
        total = jnp.dot(attention, own_w, preferred_element_type=jnp.float32)
        far_low = ring(behind[:, :half_cols], "heads", heads_n, 1)
        far_high = ring(ahead[:, half_cols:], "heads", heads_n, heads_n - 1)
        total = total + jnp.dot(behind, rows_of(1), preferred_element_type=jnp.float32)
        total = total + jnp.dot(ahead, rows_of(heads_n - 1), preferred_element_type=jnp.float32)
        far = jnp.concatenate([far_low, far_high], axis=1)
        total = total + jnp.dot(far, rows_of(2), preferred_element_type=jnp.float32)
        return total.astype(jnp.bfloat16)

    return local


def split_mesh(mesh):
    devices = mesh.devices
    heads_n, seq_n = devices.shape
    core_n = 2
    y_n = len({d.coords[1] for d in devices.flat})
    z_n = seq_n // (core_n * y_n)
    sizes = (heads_n, z_n, y_n, core_n)
    return Mesh(np.asarray(devices).reshape(sizes), ("heads",) + SEQ), sizes


def solution(mesh):
    sub, sizes = split_mesh(mesh)
    return jax.shard_map(
        make_local(sizes),
        mesh=sub,
        in_specs=(
            P(SEQ, "heads"),
            P(SEQ, "heads"),
            P(SEQ, "heads"),
            P(),
            P(),
            P("heads", None),
        ),
        out_specs=P(SEQ, "heads"),
        check_vma=False,
    )
```

```python
import math

import jax
import jax.numpy as jnp
import functools

import numpy as np
from jax import lax
from jax.experimental import pallas as pl
from jax.experimental.pallas import tpu as pltpu
from jax.sharding import Mesh
from jax.sharding import PartitionSpec as P

HEAD_SIZE = 128
BLOCK_TOKENS = 64
SEQ = ("z", "y", "core")


def shift(block, axis, size, distance):
    route = [(i, i + distance) for i in range(size) if 0 <= i + distance < size]
    return lax.ppermute(block, axis, route)


def ring(block, axis, size, distance):
    return lax.ppermute(block, axis, [(i, (i + distance) % size) for i in range(size)])


def spread(table, rows, cols):
    return jnp.repeat(jnp.repeat(table, rows, axis=-2), cols, axis=-1)


def vertical_kernel(slots_ref, first_ref, q_ref, kv_hbm, key_tok_ref, acc_ref,
                    o_ref, k_buf, v_buf, sems, *, scale):
    head = pl.program_id(0)
    heads = pl.num_programs(0)
    vert_count = k_buf.shape[1] // BLOCK_TOKENS

    def block_copies(h, buf_index):
        copies = []
        for n in range(vert_count):
            slot = slots_ref[h, n]
            rows = pl.ds(n * BLOCK_TOKENS, BLOCK_TOKENS)
            for part, buf in ((0, k_buf), (1, v_buf)):
                copies.append(
                    pltpu.make_async_copy(
                        kv_hbm.at[part, slot], buf.at[buf_index, rows], sems.at[buf_index, part, n]
                    )
                )
        return copies

    current = head % 2

    @pl.when(head == 0)
    def _():
        for copy in block_copies(0, 0):
            copy.start()

    for copy in block_copies(head, current):
        copy.wait()

    @pl.when(head + 1 < heads)
    def _():
        for copy in block_copies(head + 1, 1 - current):
            copy.start()

    s = lax.dot_general(
        q_ref[0], k_buf[current], (((1,), (1,)), ((), ())), preferred_element_type=jnp.float32
    ) * scale
    query_tok = first_ref[0] + lax.broadcasted_iota(jnp.int32, (s.shape[0], 1), 0)
    s = jnp.where(key_tok_ref[0] <= query_tok, s, -jnp.inf)
    dim = q_ref.shape[-1]
    top_d = acc_ref[0, :, dim:dim + 1]
    top = jnp.maximum(top_d, jnp.max(s, axis=1, keepdims=True))
    p = jnp.exp(s - top)
    sc = jnp.exp(top_d - top)
    total = acc_ref[0, :, dim + 1:dim + 2] * sc + jnp.sum(p, axis=1, keepdims=True)
    acc = jnp.dot(p.astype(jnp.bfloat16), v_buf[current], preferred_element_type=jnp.float32)
    o_ref[...] = ((acc_ref[0, :, :dim] * sc + acc) / total).astype(o_ref.dtype)


def vertical_attention(slots, q, kv, key_tok, query_tok, top_d, tot_d, acc_d, interpret=False):
    spare = jnp.zeros(acc_d.shape[:-1] + (acc_d.shape[-1] - 2,), acc_d.dtype)
    acc_d = jnp.concatenate([acc_d, top_d, tot_d, spare], axis=-1)
    heads, rows, dim = q.shape
    keys_n = key_tok.shape[-1]
    kernel = functools.partial(vertical_kernel, scale=1.0 / math.sqrt(dim))
    grid_spec = pltpu.PrefetchScalarGridSpec(
        num_scalar_prefetch=2,
        grid=(heads,),
        in_specs=[
            pl.BlockSpec((1, rows, dim), lambda i, t, f: (i, 0, 0)),
            pl.BlockSpec(memory_space=pl.ANY),
            pl.BlockSpec((1, 1, keys_n), lambda i, t, f: (i, 0, 0)),
            pl.BlockSpec((1, rows, 2 * dim), lambda i, t, f: (i, 0, 0)),
        ],
        out_specs=pl.BlockSpec((rows, dim), lambda i, t, f: (0, i)),
        scratch_shapes=[
            pltpu.VMEM((2, keys_n, dim), kv.dtype),
            pltpu.VMEM((2, keys_n, dim), kv.dtype),
            pltpu.SemaphoreType.DMA((2, 2, keys_n // BLOCK_TOKENS)),
        ],
    )
    return pl.pallas_call(
        kernel,
        grid_spec=grid_spec,
        out_shape=jax.ShapeDtypeStruct((rows, heads * dim), jnp.bfloat16),
        interpret=interpret,
    )(slots, query_tok[:1, 0], q, kv, key_tok, acc_d)


def make_local(sizes):
    heads_n, z_n, y_n, core_n = sizes
    cycle_size = z_n * y_n * core_n

    def local(queries, keys, values, vertical, slash, out_weight):
        head_dim = HEAD_SIZE
        local_heads = queries.shape[1] // head_dim
        token_count = queries.shape[0]
        block_count = token_count // BLOCK_TOKENS
        score_scale = 1.0 / math.sqrt(head_dim)
        kv_group = lax.axis_index("heads")
        core = lax.axis_index("core")
        cycle_index = lax.axis_index(SEQ)

        vert_group = lax.dynamic_slice_in_dim(vertical, kv_group * local_heads, local_heads, 0)
        slash_group = lax.dynamic_slice_in_dim(slash, kv_group * local_heads, local_heads, 0)
        union_list = vert_group.reshape(-1)
        listed_count = union_list.shape[0]
        owner_dev = union_list // block_count
        within_dev = union_list % block_count
        paired = jnp.stack([keys, values]).reshape(2, block_count, BLOCK_TOKENS, head_dim)
        owned_here = owner_dev == cycle_index
        capacity = 2
        local_ids = jnp.arange(block_count, dtype=jnp.int32)
        owned_blocks = jnp.any(
            owned_here[None, :] & (within_dev[None, :] == local_ids[:, None]), axis=1
        )
        below = jnp.sum(
            (owned_blocks[None, :] & (local_ids[None, :] < local_ids[:, None])).astype(jnp.int32),
            axis=1,
        )
        owned_total = jnp.sum(owned_blocks.astype(jnp.int32))
        pick = jnp.stack([owned_blocks & (below == 0), owned_blocks & (below == owned_total - 1)])

        def picked(part):
            blocks = part.reshape(block_count, BLOCK_TOKENS, head_dim).astype(jnp.float32)
            chosen_blocks = jnp.where(pick[:, :, None, None], blocks[None], 0.0)
            return jnp.sum(chosen_blocks, axis=1).astype(part.dtype)

        outgoing = jnp.stack([picked(keys), picked(values)]).reshape(
            2, capacity * BLOCK_TOKENS, head_dim
        )
        same_owner = (owner_dev[:, None] == owner_dev[None, :]) & (
            union_list[None, :] < union_list[:, None]
        )
        slot_index = jnp.sum(same_owner.astype(jnp.int32), axis=1)
        arrived = lax.all_gather(outgoing, SEQ, axis=1, tiled=True)

        rows_total, width = out_weight.shape
        col_width = width // heads_n
        half_rows = rows_total // core_n
        fetched = []
        for distance in range(1, heads_n):
            dest_cols = ((kv_group + distance) % heads_n) * col_width
            piece = lax.dynamic_slice(out_weight, (core * half_rows, dest_cols), (half_rows, col_width))
            fetched.append(ring(piece, "heads", heads_n, distance))
        fetched = jnp.stack(fetched)
        sibling_w = ring(fetched, "core", core_n, 1)
        own_w = lax.dynamic_slice(out_weight, (0, kv_group * col_width), (rows_total, col_width))

        earlier = shift(paired, SEQ, cycle_size, 1)
        farther = shift(paired, SEQ, cycle_size, 2)
        context = jnp.concatenate([farther, earlier, paired], axis=1)
        context_blocks = context.shape[1]
        context_k = context[0].reshape(context_blocks * BLOCK_TOKENS, head_dim)
        context_v = context[1].reshape(context_blocks * BLOCK_TOKENS, head_dim)
        first_block = cycle_index * block_count
        query_block = first_block + jnp.arange(block_count, dtype=jnp.int32)
        key_block = first_block - (context_blocks - block_count) + jnp.arange(
            context_blocks, dtype=jnp.int32
        )
        distance_blk = query_block[:, None] - key_block[None, :]
        token_pos = jnp.arange(BLOCK_TOKENS)
        causal_tri = token_pos[None, :] <= token_pos[:, None]
        causal_ctx = jnp.tile(causal_tri, (block_count, context_blocks))

        query_heads = queries.reshape(token_count, local_heads, head_dim).transpose(1, 0, 2)
        score_diag = (
            jnp.einsum("htd,ud->htu", query_heads, context_k, preferred_element_type=jnp.float32)
            * score_scale
        )
        in_slash = jnp.any(distance_blk[None, None] == slash_group[:, :, None, None], axis=1)
        in_vert = jnp.any(key_block[None, None, :] == vert_group[:, :, None], axis=1)
        keep_blk = in_slash & (key_block >= 0)[None, None, :] & jnp.logical_not(in_vert)[:, None, :]
        whole_blk = keep_blk & (distance_blk != 0)[None]
        allow_diag = spread(whole_blk, BLOCK_TOKENS, BLOCK_TOKENS) | (
            spread(keep_blk & (distance_blk == 0)[None], BLOCK_TOKENS, BLOCK_TOKENS)
            & causal_ctx[None]
        )
        top_diag = jnp.max(jnp.where(allow_diag, score_diag, -jnp.inf), axis=2, keepdims=True)
        expo_diag = jnp.where(allow_diag, jnp.exp(score_diag - top_diag), 0.0)
        total_diag = jnp.sum(expo_diag, axis=2, keepdims=True)
        acc_diag = jnp.einsum(
            "htu,ud->htd",
            expo_diag.astype(jnp.bfloat16),
            context_v,
            preferred_element_type=jnp.float32,
        )

        arrived = arrived.reshape(2, cycle_size * capacity, BLOCK_TOKENS, head_dim)
        vert_count = vert_group.shape[1]
        slots = (owner_dev * capacity + slot_index).reshape(local_heads, vert_count)
        key_tok = (vert_group[:, :, None] * BLOCK_TOKENS + token_pos).reshape(local_heads, 1, -1)
        query_tok = (first_block * BLOCK_TOKENS + jnp.arange(token_count, dtype=jnp.int32))[:, None]
        attention = vertical_attention(
            slots.astype(jnp.int32),
            query_heads,
            arrived,
            key_tok.astype(jnp.int32),
            query_tok,
            top_diag,
            total_diag,
            acc_diag,
        )

        def rows_of(distance):
            mine, theirs = fetched[distance - 1], sibling_w[distance - 1]
            return jnp.where(
                core == 0,
                jnp.concatenate([mine, theirs], axis=0),
                jnp.concatenate([theirs, mine], axis=0),
            )

        half_cols = attention.shape[1] // 2
        behind = ring(attention, "heads", heads_n, 1)
        ahead = ring(attention, "heads", heads_n, heads_n - 1)
        total = jnp.dot(attention, own_w, preferred_element_type=jnp.float32)
        far_low = ring(behind[:, :half_cols], "heads", heads_n, 1)
        far_high = ring(ahead[:, half_cols:], "heads", heads_n, heads_n - 1)
        total = total + jnp.dot(behind, rows_of(1), preferred_element_type=jnp.float32)
        total = total + jnp.dot(ahead, rows_of(heads_n - 1), preferred_element_type=jnp.float32)
        far = jnp.concatenate([far_low, far_high], axis=1)
        total = total + jnp.dot(far, rows_of(2), preferred_element_type=jnp.float32)
        return total.astype(jnp.bfloat16)

    return local


def split_mesh(mesh):
    devices = mesh.devices
    heads_n, seq_n = devices.shape
    core_n = 2
    y_n = len({d.coords[1] for d in devices.flat})
    z_n = seq_n // (core_n * y_n)
    sizes = (heads_n, z_n, y_n, core_n)
    return Mesh(np.asarray(devices).reshape(sizes), ("heads",) + SEQ), sizes


def solution(mesh):
    sub, sizes = split_mesh(mesh)
    return jax.shard_map(
        make_local(sizes),
        mesh=sub,
        in_specs=(
            P(SEQ, "heads"),
            P(SEQ, "heads"),
            P(SEQ, "heads"),
            P(),
            P(),
            P("heads", None),
        ),
        out_specs=P(SEQ, "heads"),
        check_vma=False,
    )
```

```python
import math

import jax
import jax.numpy as jnp
import functools

import numpy as np
from jax import lax
from jax.experimental import pallas as pl
from jax.experimental.pallas import tpu as pltpu
from jax.sharding import Mesh
from jax.sharding import PartitionSpec as P

HEAD_SIZE = 128
BLOCK_TOKENS = 64
SEQ = ("z", "y", "core")


def shift(block, axis, size, distance):
    route = [(i, i + distance) for i in range(size) if 0 <= i + distance < size]
    return lax.ppermute(block, axis, route)


def ring(block, axis, size, distance):
    return lax.ppermute(block, axis, [(i, (i + distance) % size) for i in range(size)])


def spread(table, rows, cols):
    return jnp.repeat(jnp.repeat(table, rows, axis=-2), cols, axis=-1)


def vertical_kernel(slots_ref, q_ref, kv_hbm, key_tok_ref, query_tok_ref, acc_ref,
                    o_ref, k_buf, v_buf, sems, *, scale):
    head = pl.program_id(0)
    heads = pl.num_programs(0)
    vert_count = k_buf.shape[1] // BLOCK_TOKENS

    def block_copies(h, buf_index):
        copies = []
        for n in range(vert_count):
            slot = slots_ref[h, n]
            rows = pl.ds(n * BLOCK_TOKENS, BLOCK_TOKENS)
            for part, buf in ((0, k_buf), (1, v_buf)):
                copies.append(
                    pltpu.make_async_copy(
                        kv_hbm.at[part, slot], buf.at[buf_index, rows], sems.at[buf_index, part, n]
                    )
                )
        return copies

    current = head % 2

    @pl.when(head == 0)
    def _():
        for copy in block_copies(0, 0):
            copy.start()

    for copy in block_copies(head, current):
        copy.wait()

    @pl.when(head + 1 < heads)
    def _():
        for copy in block_copies(head + 1, 1 - current):
            copy.start()

    s = lax.dot_general(
        q_ref[0], k_buf[current], (((1,), (1,)), ((), ())), preferred_element_type=jnp.float32
    ) * scale
    s = jnp.where(key_tok_ref[0] <= query_tok_ref[...], s, -jnp.inf)
    dim = q_ref.shape[-1]
    top_d = acc_ref[0, :, dim:dim + 1]
    top = jnp.maximum(top_d, jnp.max(s, axis=1, keepdims=True))
    p = jnp.exp(s - top)
    sc = jnp.exp(top_d - top)
    total = acc_ref[0, :, dim + 1:dim + 2] * sc + jnp.sum(p, axis=1, keepdims=True)
    acc = jnp.dot(p.astype(jnp.bfloat16), v_buf[current], preferred_element_type=jnp.float32)
    o_ref[...] = ((acc_ref[0, :, :dim] * sc + acc) * (1.0 / total)).astype(o_ref.dtype)


def vertical_attention(slots, q, kv, key_tok, query_tok, top_d, tot_d, acc_d, interpret=False):
    spare = jnp.zeros(acc_d.shape[:-1] + (acc_d.shape[-1] - 2,), acc_d.dtype)
    acc_d = jnp.concatenate([acc_d, top_d, tot_d, spare], axis=-1)
    heads, rows, dim = q.shape
    keys_n = key_tok.shape[-1]
    kernel = functools.partial(vertical_kernel, scale=1.0 / math.sqrt(dim))
    grid_spec = pltpu.PrefetchScalarGridSpec(
        num_scalar_prefetch=1,
        grid=(heads,),
        in_specs=[
            pl.BlockSpec((1, rows, dim), lambda i, t: (i, 0, 0)),
            pl.BlockSpec(memory_space=pl.ANY),
            pl.BlockSpec((1, 1, keys_n), lambda i, t: (i, 0, 0)),
            pl.BlockSpec((rows, 1), lambda i, t: (0, 0)),
            pl.BlockSpec((1, rows, 2 * dim), lambda i, t: (i, 0, 0)),
        ],
        out_specs=pl.BlockSpec((rows, dim), lambda i, t: (0, i)),
        scratch_shapes=[
            pltpu.VMEM((2, keys_n, dim), kv.dtype),
            pltpu.VMEM((2, keys_n, dim), kv.dtype),
            pltpu.SemaphoreType.DMA((2, 2, keys_n // BLOCK_TOKENS)),
        ],
    )
    return pl.pallas_call(
        kernel,
        grid_spec=grid_spec,
        out_shape=jax.ShapeDtypeStruct((rows, heads * dim), jnp.bfloat16),
        interpret=interpret,
    )(slots, q, kv, key_tok, query_tok, acc_d)


def make_local(sizes):
    heads_n, z_n, y_n, core_n = sizes
    cycle_size = z_n * y_n * core_n

    def local(queries, keys, values, vertical, slash, out_weight):
        head_dim = HEAD_SIZE
        local_heads = queries.shape[1] // head_dim
        token_count = queries.shape[0]
        block_count = token_count // BLOCK_TOKENS
        score_scale = 1.0 / math.sqrt(head_dim)
        kv_group = lax.axis_index("heads")
        core = lax.axis_index("core")
        cycle_index = lax.axis_index(SEQ)

        vert_group = lax.dynamic_slice_in_dim(vertical, kv_group * local_heads, local_heads, 0)
        slash_group = lax.dynamic_slice_in_dim(slash, kv_group * local_heads, local_heads, 0)
        union_list = vert_group.reshape(-1)
        listed_count = union_list.shape[0]
        owner_dev = union_list // block_count
        within_dev = union_list % block_count
        paired = jnp.stack([keys, values]).reshape(2, block_count, BLOCK_TOKENS, head_dim)
        owned_here = owner_dev == cycle_index
        capacity = 2
        local_ids = jnp.arange(block_count, dtype=jnp.int32)
        owned_blocks = jnp.any(
            owned_here[None, :] & (within_dev[None, :] == local_ids[:, None]), axis=1
        )
        below = jnp.sum(
            (owned_blocks[None, :] & (local_ids[None, :] < local_ids[:, None])).astype(jnp.int32),
            axis=1,
        )
        owned_total = jnp.sum(owned_blocks.astype(jnp.int32))
        pick = jnp.stack([owned_blocks & (below == 0), owned_blocks & (below == owned_total - 1)])

        def picked(part):
            blocks = part.reshape(block_count, BLOCK_TOKENS, head_dim).astype(jnp.float32)
            chosen_blocks = jnp.where(pick[:, :, None, None], blocks[None], 0.0)
            return jnp.sum(chosen_blocks, axis=1).astype(part.dtype)

        outgoing = jnp.stack([picked(keys), picked(values)]).reshape(
            2, capacity * BLOCK_TOKENS, head_dim
        )
        same_owner = (owner_dev[:, None] == owner_dev[None, :]) & (
            union_list[None, :] < union_list[:, None]
        )
        slot_index = jnp.sum(same_owner.astype(jnp.int32), axis=1)
        arrived = lax.all_gather(outgoing, SEQ, axis=1, tiled=True)

        rows_total, width = out_weight.shape
        col_width = width // heads_n
        half_rows = rows_total // core_n
        fetched = []
        for distance in range(1, heads_n):
            dest_cols = ((kv_group + distance) % heads_n) * col_width
            piece = lax.dynamic_slice(out_weight, (core * half_rows, dest_cols), (half_rows, col_width))
            fetched.append(ring(piece, "heads", heads_n, distance))
        fetched = jnp.stack(fetched)
        sibling_w = ring(fetched, "core", core_n, 1)
        own_w = lax.dynamic_slice(out_weight, (0, kv_group * col_width), (rows_total, col_width))

        earlier = shift(paired, SEQ, cycle_size, 1)
        farther = shift(paired, SEQ, cycle_size, 2)
        context = jnp.concatenate([farther, earlier, paired], axis=1)
        context_blocks = context.shape[1]
        context_k = context[0].reshape(context_blocks * BLOCK_TOKENS, head_dim)
        context_v = context[1].reshape(context_blocks * BLOCK_TOKENS, head_dim)
        first_block = cycle_index * block_count
        query_block = first_block + jnp.arange(block_count, dtype=jnp.int32)
        key_block = first_block - (context_blocks - block_count) + jnp.arange(
            context_blocks, dtype=jnp.int32
        )
        distance_blk = query_block[:, None] - key_block[None, :]
        token_pos = jnp.arange(BLOCK_TOKENS)
        causal_tri = token_pos[None, :] <= token_pos[:, None]
        causal_ctx = jnp.tile(causal_tri, (block_count, context_blocks))

        query_heads = queries.reshape(token_count, local_heads, head_dim).transpose(1, 0, 2)
        score_diag = (
            jnp.einsum("htd,ud->htu", query_heads, context_k, preferred_element_type=jnp.float32)
            * score_scale
        )
        in_slash = jnp.any(distance_blk[None, None] == slash_group[:, :, None, None], axis=1)
        in_vert = jnp.any(key_block[None, None, :] == vert_group[:, :, None], axis=1)
        keep_blk = in_slash & (key_block >= 0)[None, None, :] & jnp.logical_not(in_vert)[:, None, :]
        whole_blk = keep_blk & (distance_blk != 0)[None]
        allow_diag = spread(whole_blk, BLOCK_TOKENS, BLOCK_TOKENS) | (
            spread(keep_blk & (distance_blk == 0)[None], BLOCK_TOKENS, BLOCK_TOKENS)
            & causal_ctx[None]
        )
        top_diag = jnp.max(jnp.where(allow_diag, score_diag, -jnp.inf), axis=2, keepdims=True)
        expo_diag = jnp.where(allow_diag, jnp.exp(score_diag - top_diag), 0.0)
        total_diag = jnp.sum(expo_diag, axis=2, keepdims=True)
        acc_diag = jnp.einsum(
            "htu,ud->htd",
            expo_diag.astype(jnp.bfloat16),
            context_v,
            preferred_element_type=jnp.float32,
        )

        arrived = arrived.reshape(2, cycle_size * capacity, BLOCK_TOKENS, head_dim)
        vert_count = vert_group.shape[1]
        slots = (owner_dev * capacity + slot_index).reshape(local_heads, vert_count)
        key_tok = (vert_group[:, :, None] * BLOCK_TOKENS + token_pos).reshape(local_heads, 1, -1)
        query_tok = (first_block * BLOCK_TOKENS + jnp.arange(token_count, dtype=jnp.int32))[:, None]
        attention = vertical_attention(
            slots.astype(jnp.int32),
            query_heads,
            arrived,
            key_tok.astype(jnp.int32),
            query_tok,
            top_diag,
            total_diag,
            acc_diag,
        )

        def rows_of(distance):
            mine, theirs = fetched[distance - 1], sibling_w[distance - 1]
            return jnp.where(
                core == 0,
                jnp.concatenate([mine, theirs], axis=0),
                jnp.concatenate([theirs, mine], axis=0),
            )

        half_cols = attention.shape[1] // 2
        behind = ring(attention, "heads", heads_n, 1)
        ahead = ring(attention, "heads", heads_n, heads_n - 1)
        total = jnp.dot(attention, own_w, preferred_element_type=jnp.float32)
        far_low = ring(behind[:, :half_cols], "heads", heads_n, 1)
        far_high = ring(ahead[:, half_cols:], "heads", heads_n, heads_n - 1)
        total = total + jnp.dot(behind, rows_of(1), preferred_element_type=jnp.float32)
        total = total + jnp.dot(ahead, rows_of(heads_n - 1), preferred_element_type=jnp.float32)
        far = jnp.concatenate([far_low, far_high], axis=1)
        total = total + jnp.dot(far, rows_of(2), preferred_element_type=jnp.float32)
        return total.astype(jnp.bfloat16)

    return local


def split_mesh(mesh):
    devices = mesh.devices
    heads_n, seq_n = devices.shape
    core_n = 2
    y_n = len({d.coords[1] for d in devices.flat})
    z_n = seq_n // (core_n * y_n)
    sizes = (heads_n, z_n, y_n, core_n)
    return Mesh(np.asarray(devices).reshape(sizes), ("heads",) + SEQ), sizes


def solution(mesh):
    sub, sizes = split_mesh(mesh)
    return jax.shard_map(
        make_local(sizes),
        mesh=sub,
        in_specs=(
            P(SEQ, "heads"),
            P(SEQ, "heads"),
            P(SEQ, "heads"),
            P(),
            P(),
            P("heads", None),
        ),
        out_specs=P(SEQ, "heads"),
        check_vma=False,
    )
```
